128 devices in a mesh: seq: 32 (over x, z, core), tp: 4 (over y).
Axes of the slice: x: 4, y: 4, z: 4, core: 2. Of those that a mesh axis runs over, the one named last changes fastest.
Arguments:
- tokens: bfloat16 [8192, 2048], P('seq'), may hold values from -6 to 6
- norm_gain: float32 [2048], replicated, may hold values from 0.1 to 1.9
- qkv_weight: bfloat16 [2048, 4096], P(None, 'tp'), may hold values from -0.125 to 0.125
- conv_weight: float32 [4, 4096], P(None, 'tp'), may hold values from -3 to 3
- gate_down: bfloat16 [2048, 16], replicated, may hold values from -0.125 to 0.125
- gate_up: bfloat16 [16, 1024], P(None, 'tp'), may hold values from -6 to 6
- gate_bias: float32 [1024], P('tp'), may hold values from 0.3 to 8.5
- out_gate_weight: bfloat16 [2048, 2048], P(None, 'tp'), may hold values from -0.125 to 0.125
- head_gain: float32 [512], replicated, may hold values from 0.1 to 1.9
- out_weight: bfloat16 [2048, 2048], P('tp'), may hold values from -0.125 to 0.125
- final_gain: float32 [2048], replicated, may hold values from 0.1 to 1.9
- embedding: bfloat16 [32000, 2048], P(('seq', 'tp')), may hold values from -0.5 to 0.5
- lengths: int32 [8], replicated, may hold values from 1 to 4096, as said below
- packed_order: int32 [8], replicated, may hold values from 0 to 7, each once
Outputs:
- hidden: bfloat16 [8192, 2048], P('seq', 'tp')
- last_states: float32 [8, 4, 256, 512], P(None, 'tp')
- conv_edges: float32 [8, 3, 4096], P(None, None, 'tp')
- last_norms: float32 [8], replicated
- max_logits: float32 [8, 128], P(None, ('seq', 'tp'))
The draws below stay inside these ranges and needn't reach their ends.
Inputs may be any that keep to these rules, and one draw needn't show every extreme that they name: Request r of the initial order has lengths[r] tokens; the lengths sum to 8192, the largest is 4096 and the smallest is 1 or 2. packed_order names every request once; the packed positions hold the tokens of request packed_order[0], then those of packed_order[1], and so on.
All inputs are finite; a program needn't handle non-finite values.
Results may differ from the reference program's by a relative error of at most 0.015.
Values may be sent and summed in bfloat16 or wider, within the bound.
No kernel may reach another device: no remote copies, remote signals or barrier semaphores. Data moves between devices by JAX's collectives and lax.ppermute only.
A program may use at most 128 MiB of HBM per device.

```python
from functools import partial
import jax
import jax.numpy as jnp
from jax import lax

D = 2048
HEADS = 4
DK = 256
DV = 512
LOWRANK = 16
VOCAB = 32000
KCONV = 4
BLOCK = 64
REQS = 8
TOKENS = 8192
MAXLEN = 4096
CH = 4096
VSHARDS = 128
N_TP = 4


def draw_gate_bias(key, part):
    channels = HEADS * DK
    pick_key, fast_key, slow_key = jax.random.split(key, 3)
    share = 0.5
    fast_pick = jax.random.uniform(pick_key, (channels,)) < share
    fast_bias = jax.random.uniform(fast_key, (channels,), minval=0.36, maxval=0.97)
    slow_bias = jax.random.uniform(slow_key, (channels,), minval=6.0, maxval=8.5)
    return jnp.where(fast_pick, fast_bias, slow_bias).astype(jnp.float32)


def draw_lengths(key, part):
    order_key, short_key, weight_key = jax.random.split(jax.random.fold_in(key, 17), 3)
    others = REQS - 2
    shortest = jax.random.randint(short_key, (), 1, 3).astype(jnp.int32)
    remaining = (TOKENS - MAXLEN - shortest).astype(jnp.int32)
    extra = (remaining - others).astype(jnp.int32)
    weights = jax.random.randint(weight_key, (others,), 1, 101).astype(jnp.int32)
    total_weight = jnp.sum(weights).astype(jnp.int32)
    shares = (weights * extra // total_weight).astype(jnp.int32)
    leftover = (extra - jnp.sum(shares)).astype(jnp.int32)
    shares = shares.at[0].add(leftover)
    middle = (shares + 1).astype(jnp.int32)
    longest = jnp.full((1,), MAXLEN, jnp.int32)
    base = jnp.concatenate([longest, shortest[None], middle]).astype(jnp.int32)
    arrangement = jax.random.permutation(order_key, REQS)
    return base[arrangement].astype(jnp.int32)


def level_of(key, shape, shards, smallest, largest):
    factor_of, own = 1.0, jax.random.fold_in(key, 6)
    for position, shards_of in shards:
        heights = jnp.exp(jax.random.uniform(jax.random.fold_in(own, position), (shards_of,), jnp.float32, smallest / len(shards), largest / len(shards)))
        factor_of = factor_of * jnp.repeat(heights, shape[position] // shards_of).reshape([-1 if axis == position else 1 for axis in range(len(shape))])
    return factor_of


def scatter_about(own_key, shape, scale, reach, cuts=(), kind=jnp.bfloat16):
    gain = level_of(own_key, shape, cuts, -0.22, 0.18) if cuts else 1.0
    entries = jax.random.normal(own_key, shape, jnp.float32) * scale * gain
    return jnp.minimum(jnp.maximum(entries, -reach), reach).astype(kind)


def setup_inputs(seed: int = 0) -> dict:
    seeds = jax.random.split(jax.random.key(seed), 15)
    return {
        "tokens": scatter_about(seeds[0], (TOKENS, D), 1.0, 6.0, ((0, 32),)),
        "norm_gain": jnp.clip(1.0 + 0.18 * jax.random.normal(seeds[1], (D,), jnp.float32), 0.1, 1.9),
        "qkv_weight": scatter_about(seeds[2], (D, CH), D ** -0.5, 0.125, ((1, 4),)),
        "conv_weight": scatter_about(seeds[3], (KCONV, CH), KCONV ** -0.5, 3.0, ((1, 4),), jnp.float32),
        "gate_down": scatter_about(seeds[4], (D, LOWRANK), D ** -0.5, 0.125),
        "gate_up": scatter_about(seeds[5], (LOWRANK, HEADS * DK), 1.0, 6.0, ((1, 4),)),
        "gate_bias": draw_gate_bias(jax.random.fold_in(seeds[14], 71), 0),
        "out_gate_weight": scatter_about(seeds[7], (D, HEADS * DV), D ** -0.5, 0.125, ((1, 4),)),
        "head_gain": jnp.clip(1.0 + 0.18 * jax.random.normal(seeds[8], (DV,), jnp.float32), 0.1, 1.9),
        "out_weight": scatter_about(seeds[9], (HEADS * DV, D), (HEADS * DV) ** -0.5, 0.125, ((0, 4),)),
        "final_gain": jnp.clip(1.0 + 0.18 * jax.random.normal(seeds[10], (D,), jnp.float32), 0.1, 1.9),
        "embedding": scatter_about(seeds[11], (VOCAB, D), 0.08, 0.5, ((0, 128),)),
        "lengths": draw_lengths(jax.random.fold_in(seeds[14], 71), 0),
        "packed_order": jax.random.permutation(seeds[13], REQS).astype(jnp.int32),
    }


HIGHEST_PRECISION = lax.Precision.HIGHEST

def rounded(array):
    return lax.optimization_barrier(array.astype(jnp.bfloat16)).astype(jnp.float32)

def segments(lengths, packed_order, positions):
    request_count = lengths.shape[0]
    select = (packed_order[:, None] == jnp.arange(request_count, dtype=jnp.int32)[None, :]).astype(jnp.int32)
    packed_len = lax.optimization_barrier(jnp.sum(select * lengths[None, :], axis=1)).astype(jnp.int32)
    end_points = jnp.cumsum(packed_len).astype(jnp.int32)
    starts = end_points - packed_len
    segment = (lax.optimization_barrier(jnp.sum((positions[:, None] >= starts[None, :]).astype(jnp.int32), axis=1)) - 1).astype(jnp.int32)
    last_index = lax.optimization_barrier(jnp.sum(select * (end_points - 1)[:, None], axis=0)).astype(jnp.int32)
    return (segment, last_index)

def causal_conv(padded, padded_segment, conv_weight, row_count):
    running = jnp.zeros((row_count, padded.shape[1]), jnp.float32)
    current = padded_segment[KCONV - 1:]
    for offset in range(KCONV):
        window = padded[offset:offset + row_count]
        same_segment = (padded_segment[offset:offset + row_count] == current)[:, None]
        running = running + jnp.where(same_segment, window, 0.0) * conv_weight[offset]
    return running

def activate(convolved, head_count):
    shaped = convolved.reshape(convolved.shape[0], head_count, 2 * DK + DV)
    channel = jnp.arange(2 * DK + DV)
    return jnp.where(channel < 2 * DK, jax.nn.silu(shaped), shaped).astype(jnp.bfloat16)

def advance(carry_state, key_rows, values, cumulative, segment, segment_before):
    total_decay = cumulative[-1]
    same_tail = (segment == segment[-1])[:, None, None]
    scaled = rounded(jnp.where(same_tail, key_rows * jnp.exp(total_decay[None] - cumulative), 0.0))
    added = jnp.einsum('jhc,jhv->hcv', scaled, values, precision=HIGHEST_PRECISION)
    through = segment[-1] == segment_before
    return jnp.where(through, jnp.exp(total_decay)[:, :, None] * carry_state, 0.0) + added

def state_at_ends(end_states, carry_state, key_rows, values, cumulative, segment, segment_before, offset):
    length = segment.shape[0]
    inside_block = (offset >= 0) & (offset < length)

    def add_ends(previous):
        end_row = jnp.clip(offset, 0, length - 1)
        end_decay = cumulative[end_row]
        end_segment = segment[end_row]
        indices = jnp.arange(length)
        allowed = ((indices[None, :] <= end_row[:, None]) & (segment[None, :] == end_segment[:, None]))[:, :, None, None]
        spread = jnp.where(allowed, end_decay[:, None] - cumulative[None], 0.0)
        weighted = rounded(jnp.where(allowed, key_rows[None] * jnp.exp(spread), 0.0))
        within = jnp.einsum('rjhc,jhv->rhcv', weighted, values, precision=HIGHEST_PRECISION)
        carried = (end_segment == segment_before)[:, None, None, None]
        reached = jnp.where(carried, jnp.exp(end_decay)[:, :, :, None] * carry_state[None], 0.0)
        return jnp.where(inside_block[:, None, None, None], within + reached, previous)

    def keep(previous):
        return previous
    return lax.cond(jnp.any(inside_block), add_ends, keep, end_states)

def block_step(last_index, carry, inputs):
    carry_state, end_states = carry
    queries, key_rows, values, decays, segment, segment_before, block_first = inputs
    cumulative = jnp.cumsum(decays, axis=0)
    length = segment.shape[0]
    indices = jnp.arange(length)
    causal = (indices[None, :] <= indices[:, None]) & (segment[None, :] == segment[:, None])
    allowed = causal[:, :, None, None]
    spread = jnp.where(allowed, cumulative[:, None] - cumulative[None, :], 0.0)
    weights = jnp.where(allowed, jnp.exp(spread), 0.0)
    scores = rounded(lax.optimization_barrier(jnp.sum(queries[:, None] * key_rows[None, :] * weights, axis=-1)))
    inside = jnp.einsum('ijh,jhv->ihv', scores, values, precision=HIGHEST_PRECISION)
    carried = (segment == segment_before)[:, None, None]
    outside = jnp.einsum('ihc,hcv->ihv', queries * jnp.exp(cumulative), carry_state, precision=HIGHEST_PRECISION)
    output = inside + jnp.where(carried, outside, 0.0)
    new_state = advance(carry_state, key_rows, values, cumulative, segment, segment_before)
    end_states = state_at_ends(end_states, carry_state, key_rows, values, cumulative, segment, segment_before, last_index - block_first)
    return ((new_state, end_states), output)

def head_output(attended, gate_out, head_gain):
    row_count, head_count, value_width = attended.shape
    mean_square = lax.optimization_barrier(jnp.mean(attended * attended, axis=2, keepdims=True))
    gate_values = jax.nn.silu(gate_out.astype(jnp.float32).reshape(row_count, head_count, value_width))
    gated = attended * lax.rsqrt(mean_square + 1e-05) * head_gain * gate_values
    return gated.reshape(row_count, head_count * value_width).astype(jnp.bfloat16)

def reference(tokens, norm_gain, qkv_weight, conv_weight, gate_down, gate_up, gate_bias, out_gate_weight, head_gain, out_weight, final_gain, embedding, lengths, packed_order):
    row_count = tokens.shape[0]
    positions = jnp.arange(row_count, dtype=jnp.int32)
    segment, last_index = segments(lengths, packed_order, positions)
    first_index = last_index - lengths + 1
    residual = tokens.astype(jnp.float32)
    normed = (residual * lax.rsqrt(lax.optimization_barrier(jnp.mean(residual * residual, axis=1, keepdims=True)) + 1e-06) * norm_gain).astype(jnp.bfloat16)
    projected = jnp.dot(normed, qkv_weight, preferred_element_type=jnp.float32).astype(jnp.bfloat16)
    padded = jnp.concatenate([jnp.zeros((KCONV - 1, projected.shape[1]), jnp.float32), projected.astype(jnp.float32)], axis=0)
    padded_segment = jnp.concatenate([jnp.full((KCONV - 1,), -1, jnp.int32), segment.astype(jnp.int32)], axis=0)
    convolved = causal_conv(padded, padded_segment, conv_weight, row_count)
    activated = activate(convolved, HEADS)
    queries = activated[:, :, :DK].astype(jnp.float32)
    key_rows = activated[:, :, DK:2 * DK].astype(jnp.float32)
    values = activated[:, :, 2 * DK:].astype(jnp.float32)
    lowrank = jnp.dot(normed, gate_down, preferred_element_type=jnp.float32)
    gate_logits = jnp.dot(lowrank, gate_up.astype(jnp.float32), precision=HIGHEST_PRECISION) + gate_bias
    decays = (jax.nn.log_sigmoid(gate_logits) / 16.0).reshape(row_count, HEADS, DK)
    gate_out = jnp.dot(normed, out_gate_weight, preferred_element_type=jnp.float32).astype(jnp.bfloat16)
    block_count = row_count // BLOCK

    def split_blocks(array):
        return array.reshape((block_count, BLOCK) + array.shape[1:])
    segment_before = jnp.concatenate([jnp.full((1,), -1, jnp.int32), segment[:-1].astype(jnp.int32)])[::BLOCK]
    block_first = jnp.arange(block_count, dtype=jnp.int32) * BLOCK
    block_inputs = (split_blocks(queries), split_blocks(key_rows), split_blocks(values), split_blocks(decays), split_blocks(segment), segment_before, block_first)
    empty_state = jnp.zeros((HEADS, DK, DV), jnp.float32)
    empty_ends = jnp.zeros((lengths.shape[0], HEADS, DK, DV), jnp.float32)
    (ignored, last_states), attended = lax.scan(partial(block_step, last_index), (empty_state, empty_ends), block_inputs)
    attended = attended.reshape(row_count, HEADS, DV)
    gated = head_output(attended, gate_out, head_gain)
    group = HEADS * DV // N_TP
    summed = jnp.zeros((row_count, tokens.shape[1]), jnp.float32)
    for index in range(N_TP):
        partial_sum = jnp.dot(gated[:, index * group:(index + 1) * group], out_weight[index * group:(index + 1) * group], preferred_element_type=jnp.float32).astype(jnp.bfloat16)
        summed = summed + lax.optimization_barrier(partial_sum).astype(jnp.float32)
    hidden = (residual + summed).astype(jnp.bfloat16)
    edge_list = []
    for offset in range(KCONV - 1):
        located = last_index - (KCONV - 2) + offset
        inside = located >= first_index
        picked = projected[jnp.clip(located, 0, row_count - 1)].astype(jnp.float32)
        edge_list.append(jnp.where(inside[:, None], picked, 0.0))
    conv_edges = jnp.stack(edge_list, axis=1)
    last_rows = hidden[last_index].astype(jnp.float32)
    mean_square = lax.optimization_barrier(jnp.mean(last_rows * last_rows, axis=1))
    last_norms = jnp.sqrt(mean_square)
    final_rows = (last_rows * lax.rsqrt(mean_square[:, None] + 1e-06) * final_gain).astype(jnp.bfloat16)
    logits = jnp.dot(final_rows, embedding.T, preferred_element_type=jnp.float32)
    max_logits = lax.optimization_barrier(jnp.max(logits.reshape(logits.shape[0], VSHARDS, VOCAB // VSHARDS), axis=2))
    return (hidden, last_states, conv_edges, last_norms, max_logits)
```

```python
import jax
import jax.numpy as jnp
from jax import lax
from jax.sharding import PartitionSpec as P

DK = 256
DV = 512
KCONV = 4
BLOCK = 64


HIGHEST_PRECISION = lax.Precision.HIGHEST


def passed_along(array, axis, by):
    peers = lax.axis_size(axis)
    pairs = [(i, i + by) for i in range(peers) if 0 <= i + by < peers]
    return lax.ppermute(array, axis, pairs)


def butterfly_sum(array, axis):
    peers = lax.axis_size(axis)
    step = 1
    while step < peers:
        pairs = [(i, i ^ step) for i in range(peers)]
        array = array + lax.ppermute(array, axis, pairs)
        step *= 2
    return array


def state_prefix(decay_factor, local_state, axis):
    peers, place = lax.axis_size(axis), lax.axis_index(axis)
    decay = passed_along(decay_factor, axis, 1)
    state = passed_along(local_state.astype(jnp.bfloat16), axis, 1).astype(jnp.float32)
    step = 1
    while step < peers:
        earlier_decay = passed_along(decay, axis, step)
        earlier_state = passed_along(state.astype(jnp.bfloat16), axis, step).astype(jnp.float32)
        state = state + decay[..., None] * earlier_state
        decay = jnp.where(place >= step, decay * earlier_decay, decay)
        step *= 2
    return state


def segments(lengths, packed_order, positions):
    request_count = lengths.shape[0]
    select = (packed_order[:, None] == jnp.arange(request_count, dtype=jnp.int32)[None, :]).astype(
        jnp.int32
    )
    packed_len = jnp.sum(select * lengths[None, :], axis=1)
    end_points = jnp.cumsum(packed_len)
    starts = end_points - packed_len
    segment = jnp.sum((positions[:, None] >= starts[None, :]).astype(jnp.int32), axis=1) - 1
    last_index = jnp.sum(select * (end_points - 1)[:, None], axis=0)
    return (segment, last_index)


def causal_conv(padded, padded_segment, conv_weight, row_count):
    running = jnp.zeros((row_count, padded.shape[1]), jnp.float32)
    current = padded_segment[KCONV - 1 :]
    for offset in range(KCONV):
        window = padded[offset : offset + row_count]
        same_segment = (padded_segment[offset : offset + row_count] == current)[:, None]
        running = running + jnp.where(same_segment, window, 0.0) * conv_weight[offset]
    return running


def activate(convolved, head_count):
    shaped = convolved.reshape(convolved.shape[0], head_count, 2 * DK + DV)
    channel = jnp.arange(2 * DK + DV)
    return jnp.where(channel < 2 * DK, jax.nn.silu(shaped), shaped).astype(jnp.bfloat16)


def head_output(attended, gate_out, head_gain):
    row_count, head_count, value_width = attended.shape
    mean_square = jnp.mean(attended * attended, axis=2, keepdims=True)
    gate_values = jax.nn.silu(
        gate_out.astype(jnp.float32).reshape(row_count, head_count, value_width)
    )
    gated = attended * lax.rsqrt(mean_square + 1e-05) * head_gain * gate_values
    return gated.reshape(row_count, head_count * value_width).astype(jnp.bfloat16)


def shards(
    tokens,
    norm_gain,
    qkv_weight,
    conv_weight,
    gate_down,
    gate_up,
    gate_bias,
    out_gate_weight,
    head_gain,
    out_weight,
    final_gain,
    embedding,
    lengths,
    packed_order,
):
    row_count = tokens.shape[0]
    head_count = out_weight.shape[0] // DV
    tp_size = lax.axis_size("tp")
    tp_index = lax.axis_index("tp")
    column_count = tokens.shape[1] // tp_size
    request_count = lengths.shape[0]
    start_row = lax.axis_index("seq") * row_count
    positions = start_row + jnp.arange(-(KCONV - 1), row_count, dtype=jnp.int32)
    segment_all, last_index = segments(lengths, packed_order, positions)
    segment = segment_all[KCONV - 1 :]
    segment_prior = segment_all[KCONV - 2]
    first_index = last_index - lengths + 1
    residual = tokens.astype(jnp.float32)
    normed = (
        residual
        * lax.rsqrt(jnp.mean(residual * residual, axis=1, keepdims=True) + 1e-06)
        * norm_gain
    ).astype(jnp.bfloat16)
    projected = jnp.dot(normed, qkv_weight, preferred_element_type=jnp.float32).astype(jnp.bfloat16)
    rim_rows = passed_along(projected[row_count - (KCONV - 1) :], "seq", 1)
    padded = jnp.concatenate([rim_rows, projected], axis=0)
    convolved = causal_conv(padded.astype(jnp.float32), segment_all, conv_weight, row_count)
    activated = activate(convolved, head_count)
    lowrank = jnp.dot(normed, gate_down, preferred_element_type=jnp.float32)
    gate_logits = (
        jnp.dot(lowrank, gate_up.astype(jnp.float32), precision=HIGHEST_PRECISION) + gate_bias
    )
    decays = (jax.nn.log_sigmoid(gate_logits) / 16.0).reshape(row_count, head_count, DK)
    gate_out = jnp.dot(normed, out_gate_weight, preferred_element_type=jnp.float32).astype(
        jnp.bfloat16
    )

    offset = last_index - start_row
    owned_here = (offset >= 0) & (offset < row_count)
    edge_list = []
    for tap in range(KCONV - 1):
        located = last_index - (KCONV - 2) + tap
        inside = owned_here & (located >= first_index)
        picked = padded[jnp.clip(located - start_row + KCONV - 1, 0, row_count + KCONV - 2)].astype(
            jnp.float32
        )
        edge_list.append(jnp.where(inside[:, None], picked, 0.0))
    conv_edges = jnp.stack(edge_list, axis=1)

    block_count = row_count // BLOCK
    queries = activated[:, :, :DK].astype(jnp.float32).reshape(block_count, BLOCK, head_count, DK)
    key_rows = activated[:, :, DK : 2 * DK].astype(jnp.float32).reshape(
        block_count, BLOCK, head_count, DK
    )
    values = activated[:, :, 2 * DK :].reshape(block_count, BLOCK, head_count, DV)
    block_segment = segment.reshape(block_count, BLOCK)
    segment_before = segment_all[KCONV - 2 : KCONV - 2 + row_count : BLOCK]
    cumulative = jnp.cumsum(decays.reshape(block_count, BLOCK, head_count, DK), axis=1)
    indices = jnp.arange(BLOCK)
    causal = (indices[None, :] <= indices[:, None])[None] & (
        block_segment[:, None, :] == block_segment[:, :, None]
    )
    allowed = causal[:, :, :, None, None]
    spread = jnp.where(allowed, cumulative[:, :, None] - cumulative[:, None, :], 0.0)
    weights = jnp.where(allowed, jnp.exp(spread), 0.0)
    scores = jnp.sum(queries[:, :, None] * key_rows[:, None, :] * weights, axis=-1).astype(
        jnp.bfloat16
    )
    inside = jnp.einsum("bpqh,bqhv->bphv", scores, values, preferred_element_type=jnp.float32)

    same_tail = (block_segment == block_segment[:, -1:])[:, :, None, None]
    scaled = jnp.where(
        same_tail, key_rows * jnp.exp(cumulative[:, -1:] - cumulative), 0.0
    ).astype(jnp.bfloat16)
    added = jnp.einsum("bjhc,bjhv->bhcv", scaled, values, preferred_element_type=jnp.float32)
    through = block_segment[:, -1] == segment_before
    block_decay = jnp.exp(cumulative[:, -1])
    state = jnp.zeros((head_count, DK, DV), jnp.float32)
    prior = jnp.ones((head_count, DK), jnp.float32)
    states_before, priors = [], []
    for b in range(block_count):
        states_before.append(state)
        priors.append(prior)
        state = jnp.where(through[b], block_decay[b][:, :, None] * state, 0.0) + added[b]
        prior = prior * block_decay[b]
    states_before = jnp.stack(states_before)
    priors = jnp.stack(priors)
    local_state = state
    carried = (block_segment == segment_before[:, None])[:, :, None, None]
    outside = jnp.einsum(
        "bphc,bhcv->bphv", queries * jnp.exp(cumulative), states_before, precision=HIGHEST_PRECISION
    )
    attended = inside + jnp.where(carried, outside, 0.0)

    end_row = jnp.clip(offset, 0, row_count - 1)
    end_block, end_pos = end_row // BLOCK, end_row % BLOCK
    picks = jnp.arange(request_count)
    end_keys_rows = key_rows[end_block]
    end_values = values[end_block]
    end_cumulative = cumulative[end_block]
    end_segments = block_segment[end_block]
    end_decay = end_cumulative[picks, end_pos]
    end_segment = end_segments[picks, end_pos]
    end_allowed = (
        (indices[None, :] <= end_pos[:, None]) & (end_segments == end_segment[:, None])
    )[:, :, None, None]
    end_spread = jnp.where(end_allowed, end_decay[:, None] - end_cumulative, 0.0)
    end_weighted = jnp.where(end_allowed, end_keys_rows * jnp.exp(end_spread), 0.0).astype(
        jnp.bfloat16
    )
    within = jnp.einsum("rjhc,rjhv->rhcv", end_weighted, end_values, preferred_element_type=jnp.float32)
    end_carried = (end_segment == segment_before[end_block])[:, None, None, None]
    reached = jnp.where(end_carried, jnp.exp(end_decay)[:, :, :, None] * states_before[end_block], 0.0)
    local_ends = within + reached

    through_shard = segment[-1] == segment_prior
    decay_factor = jnp.where(through_shard, priors[-1] * block_decay[-1], 0.0)
    incoming = state_prefix(decay_factor, local_state, "seq")

    reach = jnp.exp(cumulative) * priors[:, None]
    from_before = (block_segment == segment_prior)[:, :, None, None]
    correction = jnp.einsum(
        "bphc,hcv->bphv",
        jnp.where(from_before, queries * reach, 0.0),
        incoming,
        precision=HIGHEST_PRECISION,
    )
    attended = (attended + correction).reshape(row_count, head_count, DV)
    end_reach = jnp.exp(end_decay) * priors[end_block]
    end_from_before = (end_segment == segment_prior)[:, None, None, None]
    end_states = local_ends + jnp.where(
        end_from_before, end_reach[:, :, :, None] * incoming[None], 0.0
    )
    end_states = jnp.where(owned_here[:, None, None, None], end_states, 0.0)
    state_width = head_count * DK * DV
    payload = jnp.concatenate(
        [end_states.reshape(request_count, state_width), conv_edges.reshape(request_count, -1)], axis=1
    )
    payload = lax.psum(payload.astype(jnp.bfloat16), "seq").astype(jnp.float32)
    last_states = payload[:, :state_width].reshape(end_states.shape)
    conv_edges = payload[:, state_width:].reshape(conv_edges.shape)

    gated = head_output(attended, gate_out, head_gain)
    partial = jnp.dot(gated, out_weight, preferred_element_type=jnp.float32).astype(jnp.bfloat16)
    pieces = partial.reshape(row_count, tp_size, column_count)
    arrived = [lax.dynamic_index_in_dim(pieces, tp_index, 1, keepdims=False)]
    for shift in range(1, tp_size):
        outgoing = lax.dynamic_index_in_dim(pieces, (tp_index + shift) % tp_size, 1, keepdims=False)
        arrived.append(
            lax.ppermute(outgoing, "tp", [(i, (i + shift) % tp_size) for i in range(tp_size)])
        )
    arrived = jnp.stack(arrived)
    summed = jnp.zeros((row_count, column_count), jnp.float32)
    for group in range(tp_size):
        summed = summed + lax.dynamic_index_in_dim(
            arrived, (tp_index - group) % tp_size, 0, keepdims=False
        ).astype(jnp.float32)
    column_start = tp_index * column_count
    own_columns = lax.dynamic_slice_in_dim(residual, column_start, column_count, 1)
    hidden = (own_columns + summed).astype(jnp.bfloat16)

    last_rows = jnp.where(owned_here[:, None], hidden[end_row], jnp.zeros((), jnp.bfloat16))
    placed = lax.dynamic_update_slice_in_dim(
        jnp.zeros((request_count, tokens.shape[1]), jnp.bfloat16), last_rows, column_start, 1
    )
    full_rows = butterfly_sum(butterfly_sum(placed, "seq"), "tp").astype(jnp.float32)
    mean_square = jnp.mean(full_rows * full_rows, axis=1)
    last_norms = jnp.sqrt(mean_square)
    final_rows = (full_rows * lax.rsqrt(mean_square[:, None] + 1e-06) * final_gain).astype(
        jnp.bfloat16
    )
    logits = jnp.dot(final_rows, embedding.T, preferred_element_type=jnp.float32)
    max_logits = jnp.max(logits, axis=1, keepdims=True)
    return (hidden, last_states, conv_edges, last_norms, max_logits)


def solution(mesh):
    in_specs = (
        P("seq", None),
        P(),
        P(None, "tp"),
        P(None, "tp"),
        P(),
        P(None, "tp"),
        P("tp"),
        P(None, "tp"),
        P(),
        P("tp", None),
        P(),
        P(("seq", "tp"), None),
        P(),
        P(),
    )
    out_specs = (
        P("seq", "tp"),
        P(None, "tp", None, None),
        P(None, None, "tp"),
        P(),
        P(None, ("seq", "tp")),
    )
    return jax.shard_map(shards, mesh=mesh, in_specs=in_specs, out_specs=out_specs, check_vma=False)
```

```python
import jax
import jax.numpy as jnp
from jax import lax
from jax.sharding import PartitionSpec as P

DK = 256
DV = 512
KCONV = 4
BLOCK = 64
MAXLEN = 4096


HIGHEST_PRECISION = lax.Precision.HIGHEST


def passed_along(array, axis, by):
    peers = lax.axis_size(axis)
    pairs = [(i, i + by) for i in range(peers) if 0 <= i + by < peers]
    return lax.ppermute(array, axis, pairs)


def butterfly_sum(array, axis):
    peers = lax.axis_size(axis)
    step = 1
    while step < peers:
        pairs = [(i, i ^ step) for i in range(peers)]
        array = array + lax.ppermute(array, axis, pairs)
        step *= 2
    return array


def state_prefix(decay_factor, local_state, axis, reach):
    peers, place = lax.axis_size(axis), lax.axis_index(axis)
    decay = passed_along(decay_factor, axis, 1)
    state = passed_along(local_state.astype(jnp.bfloat16), axis, 1).astype(jnp.float32)
    step = 1
    while step < min(peers, reach):
        earlier_decay = passed_along(decay, axis, step)
        earlier_state = passed_along(state.astype(jnp.bfloat16), axis, step).astype(jnp.float32)
        state = state + decay[..., None] * earlier_state
        decay = jnp.where(place >= step, decay * earlier_decay, decay)
        step *= 2
    return state


def segments(lengths, packed_order, positions):
    request_count = lengths.shape[0]
    select = (packed_order[:, None] == jnp.arange(request_count, dtype=jnp.int32)[None, :]).astype(
        jnp.int32
    )
    packed_len = jnp.sum(select * lengths[None, :], axis=1)
    end_points = jnp.cumsum(packed_len)
    starts = end_points - packed_len
    segment = jnp.sum((positions[:, None] >= starts[None, :]).astype(jnp.int32), axis=1) - 1
    last_index = jnp.sum(select * (end_points - 1)[:, None], axis=0)
    return (segment, last_index)


def causal_conv(padded, padded_segment, conv_weight, row_count):
    running = jnp.zeros((row_count, padded.shape[1]), jnp.float32)
    current = padded_segment[KCONV - 1 :]
    for offset in range(KCONV):
        window = padded[offset : offset + row_count]
        same_segment = (padded_segment[offset : offset + row_count] == current)[:, None]
        running = running + jnp.where(same_segment, window, 0.0) * conv_weight[offset]
    return running


def activate(convolved, head_count):
    shaped = convolved.reshape(convolved.shape[0], head_count, 2 * DK + DV)
    channel = jnp.arange(2 * DK + DV)
    return jnp.where(channel < 2 * DK, jax.nn.silu(shaped), shaped).astype(jnp.bfloat16)


def head_output(attended, gate_out, head_gain):
    row_count, head_count, value_width = attended.shape
    mean_square = jnp.mean(attended * attended, axis=2, keepdims=True)
    gate_values = jax.nn.silu(
        gate_out.astype(jnp.float32).reshape(row_count, head_count, value_width)
    )
    gated = attended * lax.rsqrt(mean_square + 1e-05) * head_gain * gate_values
    return gated.reshape(row_count, head_count * value_width).astype(jnp.bfloat16)


def shards(
    tokens,
    norm_gain,
    qkv_weight,
    conv_weight,
    gate_down,
    gate_up,
    gate_bias,
    out_gate_weight,
    head_gain,
    out_weight,
    final_gain,
    embedding,
    lengths,
    packed_order,
):
    row_count = tokens.shape[0]
    head_count = out_weight.shape[0] // DV
    tp_size = lax.axis_size("tp")
    tp_index = lax.axis_index("tp")
    column_count = tokens.shape[1] // tp_size
    request_count = lengths.shape[0]
    start_row = lax.axis_index("seq") * row_count
    positions = start_row + jnp.arange(-(KCONV - 1), row_count, dtype=jnp.int32)
    segment_all, last_index = segments(lengths, packed_order, positions)
    segment = segment_all[KCONV - 1 :]
    segment_prior = segment_all[KCONV - 2]
    first_index = last_index - lengths + 1
    residual = tokens.astype(jnp.float32)
    normed = (
        residual
        * lax.rsqrt(jnp.mean(residual * residual, axis=1, keepdims=True) + 1e-06)
        * norm_gain
    ).astype(jnp.bfloat16)
    projected = jnp.dot(normed, qkv_weight, preferred_element_type=jnp.float32).astype(jnp.bfloat16)
    rim_rows = passed_along(projected[row_count - (KCONV - 1) :], "seq", 1)
    padded = jnp.concatenate([rim_rows, projected], axis=0)
    convolved = causal_conv(padded.astype(jnp.float32), segment_all, conv_weight, row_count)
    activated = activate(convolved, head_count)
    lowrank = jnp.dot(normed, gate_down, preferred_element_type=jnp.float32)
    gate_logits = (
        jnp.dot(lowrank, gate_up.astype(jnp.float32), precision=HIGHEST_PRECISION) + gate_bias
    )
    decays = (jax.nn.log_sigmoid(gate_logits) / 16.0).reshape(row_count, head_count, DK)
    gate_out = jnp.dot(normed, out_gate_weight, preferred_element_type=jnp.float32).astype(
        jnp.bfloat16
    )

    offset = last_index - start_row
    owned_here = (offset >= 0) & (offset < row_count)
    edge_list = []
    for tap in range(KCONV - 1):
        located = last_index - (KCONV - 2) + tap
        inside = owned_here & (located >= first_index)
        picked = padded[jnp.clip(located - start_row + KCONV - 1, 0, row_count + KCONV - 2)].astype(
            jnp.float32
        )
        edge_list.append(jnp.where(inside[:, None], picked, 0.0))
    conv_edges = jnp.stack(edge_list, axis=1)

    block_count = row_count // BLOCK
    queries = activated[:, :, :DK].astype(jnp.float32).reshape(block_count, BLOCK, head_count, DK)
    key_rows = activated[:, :, DK : 2 * DK].astype(jnp.float32).reshape(
        block_count, BLOCK, head_count, DK
    )
    values = activated[:, :, 2 * DK :].reshape(block_count, BLOCK, head_count, DV)
    block_segment = segment.reshape(block_count, BLOCK)
    segment_before = segment_all[KCONV - 2 : KCONV - 2 + row_count : BLOCK]
    cumulative = jnp.cumsum(decays.reshape(block_count, BLOCK, head_count, DK), axis=1)
    indices = jnp.arange(BLOCK)
    causal = (indices[None, :] <= indices[:, None])[None] & (
        block_segment[:, None, :] == block_segment[:, :, None]
    )
    allowed = causal[:, :, :, None, None]
    spread = jnp.where(allowed, cumulative[:, :, None] - cumulative[:, None, :], 0.0)
    weights = jnp.where(allowed, jnp.exp(spread), 0.0)
    scores = jnp.sum(queries[:, :, None] * key_rows[:, None, :] * weights, axis=-1).astype(
        jnp.bfloat16
    )
    inside = jnp.einsum("bpqh,bqhv->bphv", scores, values, preferred_element_type=jnp.float32)

    same_tail = (block_segment == block_segment[:, -1:])[:, :, None, None]
    scaled = jnp.where(
        same_tail, key_rows * jnp.exp(cumulative[:, -1:] - cumulative), 0.0
    ).astype(jnp.bfloat16)
    added = jnp.einsum("bjhc,bjhv->bhcv", scaled, values, preferred_element_type=jnp.float32)
    through = block_segment[:, -1] == segment_before
    block_decay = jnp.exp(cumulative[:, -1])
    state = jnp.zeros((head_count, DK, DV), jnp.float32)
    prior = jnp.ones((head_count, DK), jnp.float32)
    states_before, priors = [], []
    for b in range(block_count):
        states_before.append(state)
        priors.append(prior)
        state = jnp.where(through[b], block_decay[b][:, :, None] * state, 0.0) + added[b]
        prior = prior * block_decay[b]
    states_before = jnp.stack(states_before)
    priors = jnp.stack(priors)
    local_state = state
    carried = (block_segment == segment_before[:, None])[:, :, None, None]
    outside = jnp.einsum(
        "bphc,bhcv->bphv", queries * jnp.exp(cumulative), states_before, precision=HIGHEST_PRECISION
    )
    attended = inside + jnp.where(carried, outside, 0.0)

    end_row = jnp.clip(offset, 0, row_count - 1)
    end_block, end_pos = end_row // BLOCK, end_row % BLOCK
    picks = jnp.arange(request_count)
    end_keys_rows = key_rows[end_block]
    end_values = values[end_block]
    end_cumulative = cumulative[end_block]
    end_segments = block_segment[end_block]
    end_decay = end_cumulative[picks, end_pos]
    end_segment = end_segments[picks, end_pos]
    end_allowed = (
        (indices[None, :] <= end_pos[:, None]) & (end_segments == end_segment[:, None])
    )[:, :, None, None]
    end_spread = jnp.where(end_allowed, end_decay[:, None] - end_cumulative, 0.0)
    end_weighted = jnp.where(end_allowed, end_keys_rows * jnp.exp(end_spread), 0.0).astype(
        jnp.bfloat16
    )
    within = jnp.einsum("rjhc,rjhv->rhcv", end_weighted, end_values, preferred_element_type=jnp.float32)
    end_carried = (end_segment == segment_before[end_block])[:, None, None, None]
    reached = jnp.where(end_carried, jnp.exp(end_decay)[:, :, :, None] * states_before[end_block], 0.0)
    local_ends = within + reached

    seq_size, seq_index = lax.axis_size("seq"), lax.axis_index("seq")
    through_shard = segment[-1] == segment_prior
    decay_factor = jnp.where(through_shard, priors[-1] * block_decay[-1], 0.0)
    end_reach = jnp.exp(end_decay) * priors[end_block]
    end_from_before = end_segment == segment_prior
    reach_here = jnp.where((owned_here & end_from_before)[:, None, None], end_reach, 0.0)
    table = jnp.concatenate(
        [
            jnp.where((jnp.arange(seq_size) == seq_index)[:, None, None], decay_factor[None], 0.0),
            reach_here,
        ]
    )
    table = butterfly_sum(table, "seq")
    shard_decays, end_reaches = table[:seq_size], table[seq_size:]
    end_shard = last_index // row_count
    shard_ids = jnp.arange(seq_size)
    between = (shard_ids[None, :] > seq_index) & (shard_ids[None, :] < end_shard[:, None])
    spanned = jnp.prod(
        jnp.where(between[:, :, None, None], shard_decays[None], 1.0), axis=1
    )
    from_here = (seq_index < end_shard)[:, None, None, None]
    end_terms = jnp.where(owned_here[:, None, None, None], local_ends, 0.0) + jnp.where(
        from_here, (end_reaches * spanned)[:, :, :, None] * local_state[None], 0.0
    )
    state_width = head_count * DK * DV
    payload = jnp.concatenate(
        [end_terms.reshape(request_count, state_width), conv_edges.reshape(request_count, -1)], axis=1
    )
    payload = lax.psum(payload.astype(jnp.bfloat16), "seq").astype(jnp.float32)

    incoming = state_prefix(decay_factor, local_state, "seq", -(-MAXLEN // row_count))
    payload, incoming = lax.optimization_barrier((payload, incoming))
    last_states = payload[:, :state_width].reshape(local_ends.shape)
    conv_edges = payload[:, state_width:].reshape(conv_edges.shape)
    reach = jnp.exp(cumulative) * priors[:, None]
    from_before = (block_segment == segment_prior)[:, :, None, None]
    correction = jnp.einsum(
        "bphc,hcv->bphv",
        jnp.where(from_before, queries * reach, 0.0),
        incoming,
        precision=HIGHEST_PRECISION,
    )
    attended = (attended + correction).reshape(row_count, head_count, DV)

    gated = head_output(attended, gate_out, head_gain)
    partial = jnp.dot(gated, out_weight, preferred_element_type=jnp.float32).astype(jnp.bfloat16)
    pieces = partial.reshape(row_count, tp_size, column_count)
    arrived = [lax.dynamic_index_in_dim(pieces, tp_index, 1, keepdims=False)]
    for shift in range(1, tp_size):
        outgoing = lax.dynamic_index_in_dim(pieces, (tp_index + shift) % tp_size, 1, keepdims=False)
        arrived.append(
            lax.ppermute(outgoing, "tp", [(i, (i + shift) % tp_size) for i in range(tp_size)])
        )
    arrived = jnp.stack(arrived)
    summed = jnp.zeros((row_count, column_count), jnp.float32)
    for group in range(tp_size):
        summed = summed + lax.dynamic_index_in_dim(
            arrived, (tp_index - group) % tp_size, 0, keepdims=False
        ).astype(jnp.float32)
    column_start = tp_index * column_count
    own_columns = lax.dynamic_slice_in_dim(residual, column_start, column_count, 1)
    hidden = (own_columns + summed).astype(jnp.bfloat16)

    last_rows = jnp.where(owned_here[:, None], hidden[end_row], jnp.zeros((), jnp.bfloat16))
    placed = lax.dynamic_update_slice_in_dim(
        jnp.zeros((request_count, tokens.shape[1]), jnp.bfloat16), last_rows, column_start, 1
    )
    full_rows = butterfly_sum(butterfly_sum(placed, "seq"), "tp").astype(jnp.float32)
    mean_square = jnp.mean(full_rows * full_rows, axis=1)
    last_norms = jnp.sqrt(mean_square)
    final_rows = (full_rows * lax.rsqrt(mean_square[:, None] + 1e-06) * final_gain).astype(
        jnp.bfloat16
    )
    logits = jnp.dot(final_rows, embedding.T, preferred_element_type=jnp.float32)
    max_logits = jnp.max(logits, axis=1, keepdims=True)
    return (hidden, last_states, conv_edges, last_norms, max_logits)


def solution(mesh):
    in_specs = (
        P("seq", None),
        P(),
        P(None, "tp"),
        P(None, "tp"),
        P(),
        P(None, "tp"),
        P("tp"),
        P(None, "tp"),
        P(),
        P("tp", None),
        P(),
        P(("seq", "tp"), None),
        P(),
        P(),
    )
    out_specs = (
        P("seq", "tp"),
        P(None, "tp", None, None),
        P(None, None, "tp"),
        P(),
        P(None, ("seq", "tp")),
    )
    return jax.shard_map(shards, mesh=mesh, in_specs=in_specs, out_specs=out_specs, check_vma=False)
```

```python
import jax
import jax.numpy as jnp
from jax import lax
from jax.sharding import PartitionSpec as P

DK = 256
DV = 512
KCONV = 4
BLOCK = 64
MAXLEN = 4096


HIGHEST_PRECISION = lax.Precision.HIGHEST


def passed_along(array, axis, by):
    peers = lax.axis_size(axis)
    pairs = [(i, i + by) for i in range(peers) if 0 <= i + by < peers]
    return lax.ppermute(array, axis, pairs)


def butterfly_sum(array, axis):
    peers = lax.axis_size(axis)
    step = 1
    while step < peers:
        pairs = [(i, i ^ step) for i in range(peers)]
        array = array + lax.ppermute(array, axis, pairs)
        step *= 2
    return array


def send_pair(decay, state, axis, by):
    high = decay.astype(jnp.bfloat16)
    low = (decay - high.astype(jnp.float32)).astype(jnp.bfloat16)
    row = jnp.concatenate([high, low], axis=-1)[:, None, :]
    packed = jnp.concatenate([state.astype(jnp.bfloat16), row], axis=1)
    got = passed_along(packed, axis, by)
    tail = got[:, DK].astype(jnp.float32)
    return tail[:, :DK] + tail[:, DK:], got[:, :DK].astype(jnp.float32)


def state_prefix(decay_factor, local_state, axis, reach):
    peers, place = lax.axis_size(axis), lax.axis_index(axis)
    decay, state = send_pair(decay_factor, local_state, axis, 1)
    step = 1
    while step < min(peers, reach):
        earlier_decay, earlier_state = send_pair(decay, state, axis, step)
        state = state + decay[..., None] * earlier_state
        decay = jnp.where(place >= step, decay * earlier_decay, decay)
        step *= 2
    return state


def segments(lengths, packed_order, positions):
    request_count = lengths.shape[0]
    select = (packed_order[:, None] == jnp.arange(request_count, dtype=jnp.int32)[None, :]).astype(
        jnp.int32
    )
    packed_len = jnp.sum(select * lengths[None, :], axis=1)
    end_points = jnp.cumsum(packed_len)
    starts = end_points - packed_len
    segment = jnp.sum((positions[:, None] >= starts[None, :]).astype(jnp.int32), axis=1) - 1
    last_index = jnp.sum(select * (end_points - 1)[:, None], axis=0)
    return (segment, last_index)


def causal_conv(padded, padded_segment, conv_weight, row_count):
    running = jnp.zeros((row_count, padded.shape[1]), jnp.float32)
    current = padded_segment[KCONV - 1 :]
    for offset in range(KCONV):
        window = padded[offset : offset + row_count]
        same_segment = (padded_segment[offset : offset + row_count] == current)[:, None]
        running = running + jnp.where(same_segment, window, 0.0) * conv_weight[offset]
    return running


def activate(convolved, head_count):
    shaped = convolved.reshape(convolved.shape[0], head_count, 2 * DK + DV)
    channel = jnp.arange(2 * DK + DV)
    return jnp.where(channel < 2 * DK, jax.nn.silu(shaped), shaped).astype(jnp.bfloat16)


def head_output(attended, gate_out, head_gain):
    row_count, head_count, value_width = attended.shape
    mean_square = jnp.mean(attended * attended, axis=2, keepdims=True)
    gate_values = jax.nn.silu(
        gate_out.astype(jnp.float32).reshape(row_count, head_count, value_width)
    )
    gated = attended * lax.rsqrt(mean_square + 1e-05) * head_gain * gate_values
    return gated.reshape(row_count, head_count * value_width).astype(jnp.bfloat16)


def shards(
    tokens,
    norm_gain,
    qkv_weight,
    conv_weight,
    gate_down,
    gate_up,
    gate_bias,
    out_gate_weight,
    head_gain,
    out_weight,
    final_gain,
    embedding,
    lengths,
    packed_order,
):
    row_count = tokens.shape[0]
    head_count = out_weight.shape[0] // DV
    tp_size = lax.axis_size("tp")
    tp_index = lax.axis_index("tp")
    column_count = tokens.shape[1] // tp_size
    request_count = lengths.shape[0]
    start_row = lax.axis_index("seq") * row_count
    positions = start_row + jnp.arange(-(KCONV - 1), row_count, dtype=jnp.int32)
    segment_all, last_index = segments(lengths, packed_order, positions)
    segment = segment_all[KCONV - 1 :]
    segment_prior = segment_all[KCONV - 2]
    first_index = last_index - lengths + 1
    residual = tokens.astype(jnp.float32)
    normed = (
        residual
        * lax.rsqrt(jnp.mean(residual * residual, axis=1, keepdims=True) + 1e-06)
        * norm_gain
    ).astype(jnp.bfloat16)
    projected = jnp.dot(normed, qkv_weight, preferred_element_type=jnp.float32).astype(jnp.bfloat16)
    rim_rows = passed_along(projected[row_count - (KCONV - 1) :], "seq", 1)
    padded = jnp.concatenate([rim_rows, projected], axis=0)
    convolved = causal_conv(padded.astype(jnp.float32), segment_all, conv_weight, row_count)
    activated = activate(convolved, head_count)
    lowrank = jnp.dot(normed, gate_down, preferred_element_type=jnp.float32)
    gate_logits = (
        jnp.dot(lowrank, gate_up.astype(jnp.float32), precision=HIGHEST_PRECISION) + gate_bias
    )
    decays = (jax.nn.log_sigmoid(gate_logits) / 16.0).reshape(row_count, head_count, DK)
    gate_out = jnp.dot(normed, out_gate_weight, preferred_element_type=jnp.float32).astype(
        jnp.bfloat16
    )

    offset = last_index - start_row
    owned_here = (offset >= 0) & (offset < row_count)
    edge_list = []
    for tap in range(KCONV - 1):
        located = last_index - (KCONV - 2) + tap
        inside = owned_here & (located >= first_index)
        picked = padded[jnp.clip(located - start_row + KCONV - 1, 0, row_count + KCONV - 2)].astype(
            jnp.float32
        )
        edge_list.append(jnp.where(inside[:, None], picked, 0.0))
    conv_edges = jnp.stack(edge_list, axis=1)

    block_count = row_count // BLOCK
    queries = activated[:, :, :DK].astype(jnp.float32).reshape(block_count, BLOCK, head_count, DK)
    key_rows = activated[:, :, DK : 2 * DK].astype(jnp.float32).reshape(
        block_count, BLOCK, head_count, DK
    )
    values = activated[:, :, 2 * DK :].reshape(block_count, BLOCK, head_count, DV)
    block_segment = segment.reshape(block_count, BLOCK)
    segment_before = segment_all[KCONV - 2 : KCONV - 2 + row_count : BLOCK]
    cumulative = jnp.cumsum(decays.reshape(block_count, BLOCK, head_count, DK), axis=1)
    indices = jnp.arange(BLOCK)
    causal = (indices[None, :] <= indices[:, None])[None] & (
        block_segment[:, None, :] == block_segment[:, :, None]
    )
    allowed = causal[:, :, :, None, None]
    spread = jnp.where(allowed, cumulative[:, :, None] - cumulative[:, None, :], 0.0)
    weights = jnp.where(allowed, jnp.exp(spread), 0.0)
    scores = jnp.sum(queries[:, :, None] * key_rows[:, None, :] * weights, axis=-1).astype(
        jnp.bfloat16
    )
    inside = jnp.einsum("bpqh,bqhv->bphv", scores, values, preferred_element_type=jnp.float32)

    same_tail = (block_segment == block_segment[:, -1:])[:, :, None, None]
    scaled = jnp.where(
        same_tail, key_rows * jnp.exp(cumulative[:, -1:] - cumulative), 0.0
    ).astype(jnp.bfloat16)
    added = jnp.einsum("bjhc,bjhv->bhcv", scaled, values, preferred_element_type=jnp.float32)
    through = block_segment[:, -1] == segment_before
    block_decay = jnp.exp(cumulative[:, -1])
    state = jnp.zeros((head_count, DK, DV), jnp.float32)
    prior = jnp.ones((head_count, DK), jnp.float32)
    states_before, priors = [], []
    for b in range(block_count):
        states_before.append(state)
        priors.append(prior)
        state = jnp.where(through[b], block_decay[b][:, :, None] * state, 0.0) + added[b]
        prior = prior * block_decay[b]
    states_before = jnp.stack(states_before)
    priors = jnp.stack(priors)
    local_state = state
    carried = (block_segment == segment_before[:, None])[:, :, None, None]
    outside = jnp.einsum(
        "bphc,bhcv->bphv", queries * jnp.exp(cumulative), states_before, precision=HIGHEST_PRECISION
    )
    attended = inside + jnp.where(carried, outside, 0.0)

    end_row = jnp.clip(offset, 0, row_count - 1)
    end_block, end_pos = end_row // BLOCK, end_row % BLOCK
    picks = jnp.arange(request_count)
    end_keys_rows = key_rows[end_block]
    end_values = values[end_block]
    end_cumulative = cumulative[end_block]
    end_segments = block_segment[end_block]
    end_decay = end_cumulative[picks, end_pos]
    end_segment = end_segments[picks, end_pos]
    end_allowed = (
        (indices[None, :] <= end_pos[:, None]) & (end_segments == end_segment[:, None])
    )[:, :, None, None]
    end_spread = jnp.where(end_allowed, end_decay[:, None] - end_cumulative, 0.0)
    end_weighted = jnp.where(end_allowed, end_keys_rows * jnp.exp(end_spread), 0.0).astype(
        jnp.bfloat16
    )
    within = jnp.einsum("rjhc,rjhv->rhcv", end_weighted, end_values, preferred_element_type=jnp.float32)
    end_carried = (end_segment == segment_before[end_block])[:, None, None, None]
    reached = jnp.where(end_carried, jnp.exp(end_decay)[:, :, :, None] * states_before[end_block], 0.0)
    local_ends = within + reached

    through_shard = segment[-1] == segment_prior
    decay_factor = jnp.where(through_shard, priors[-1] * block_decay[-1], 0.0)
    incoming = state_prefix(decay_factor, local_state, "seq", -(-MAXLEN // row_count))

    reach = jnp.exp(cumulative) * priors[:, None]
    from_before = (block_segment == segment_prior)[:, :, None, None]
    correction = jnp.einsum(
        "bphc,hcv->bphv",
        jnp.where(from_before, queries * reach, 0.0),
        incoming,
        precision=HIGHEST_PRECISION,
    )
    attended = (attended + correction).reshape(row_count, head_count, DV)
    end_reach = jnp.exp(end_decay) * priors[end_block]
    end_from_before = (end_segment == segment_prior)[:, None, None, None]
    end_states = local_ends + jnp.where(
        end_from_before, end_reach[:, :, :, None] * incoming[None], 0.0
    )
    end_states = jnp.where(owned_here[:, None, None, None], end_states, 0.0)
    state_width = head_count * DK * DV
    payload = jnp.concatenate(
        [end_states.reshape(request_count, state_width), conv_edges.reshape(request_count, -1)], axis=1
    )
    payload = lax.psum(payload.astype(jnp.bfloat16), "seq").astype(jnp.float32)
    last_states = payload[:, :state_width].reshape(end_states.shape)
    conv_edges = payload[:, state_width:].reshape(conv_edges.shape)

    gated = head_output(attended, gate_out, head_gain)
    partial = jnp.dot(gated, out_weight, preferred_element_type=jnp.float32).astype(jnp.bfloat16)
    pieces = partial.reshape(row_count, tp_size, column_count)
    arrived = [lax.dynamic_index_in_dim(pieces, tp_index, 1, keepdims=False)]
    for shift in range(1, tp_size):
        outgoing = lax.dynamic_index_in_dim(pieces, (tp_index + shift) % tp_size, 1, keepdims=False)
        arrived.append(
            lax.ppermute(outgoing, "tp", [(i, (i + shift) % tp_size) for i in range(tp_size)])
        )
    arrived = jnp.stack(arrived)
    summed = jnp.zeros((row_count, column_count), jnp.float32)
    for group in range(tp_size):
        summed = summed + lax.dynamic_index_in_dim(
            arrived, (tp_index - group) % tp_size, 0, keepdims=False
        ).astype(jnp.float32)
    column_start = tp_index * column_count
    own_columns = lax.dynamic_slice_in_dim(residual, column_start, column_count, 1)
    hidden = (own_columns + summed).astype(jnp.bfloat16)

    last_rows = jnp.where(owned_here[:, None], hidden[end_row], jnp.zeros((), jnp.bfloat16))
    placed = lax.dynamic_update_slice_in_dim(
        jnp.zeros((request_count, tokens.shape[1]), jnp.bfloat16), last_rows, column_start, 1
    )
    full_rows = butterfly_sum(butterfly_sum(placed, "seq"), "tp").astype(jnp.float32)
    mean_square = jnp.mean(full_rows * full_rows, axis=1)
    last_norms = jnp.sqrt(mean_square)
    final_rows = (full_rows * lax.rsqrt(mean_square[:, None] + 1e-06) * final_gain).astype(
        jnp.bfloat16
    )
    logits = jnp.dot(final_rows, embedding.T, preferred_element_type=jnp.float32)
    max_logits = jnp.max(logits, axis=1, keepdims=True)
    return (hidden, last_states, conv_edges, last_norms, max_logits)


def solution(mesh):
    in_specs = (
        P("seq", None),
        P(),
        P(None, "tp"),
        P(None, "tp"),
        P(),
        P(None, "tp"),
        P("tp"),
        P(None, "tp"),
        P(),
        P("tp", None),
        P(),
        P(("seq", "tp"), None),
        P(),
        P(),
    )
    out_specs = (
        P("seq", "tp"),
        P(None, "tp", None, None),
        P(None, None, "tp"),
        P(),
        P(None, ("seq", "tp")),
    )
    return jax.shard_map(shards, mesh=mesh, in_specs=in_specs, out_specs=out_specs, check_vma=False)
```

```python
import jax
import jax.numpy as jnp
from jax import lax
from jax.sharding import PartitionSpec as P

DK = 256
DV = 512
KCONV = 4
BLOCK = 64
MAXLEN = 4096


HIGHEST_PRECISION = lax.Precision.HIGHEST


def passed_along(array, axis, by):
    peers = lax.axis_size(axis)
    pairs = [(i, i + by) for i in range(peers) if 0 <= i + by < peers]
    return lax.ppermute(array, axis, pairs)


def butterfly_sum(array, axis):
    peers = lax.axis_size(axis)
    step = 1
    while step < peers:
        radix = 4 if peers % (step * 4) == 0 else 2
        total = array
        for digit in range(1, radix):
            pairs = [(i, i ^ (digit * step)) for i in range(peers)]
            total = total + lax.ppermute(array, axis, pairs)
        array = total
        step *= radix
    return array


def send_pair(decay, state, axis, by):
    high = decay.astype(jnp.bfloat16)
    low = (decay - high.astype(jnp.float32)).astype(jnp.bfloat16)
    row = jnp.concatenate([high, low], axis=-1)[:, None, :]
    packed = jnp.concatenate([state.astype(jnp.bfloat16), row], axis=1)
    got = passed_along(packed, axis, by)
    tail = got[:, DK].astype(jnp.float32)
    return tail[:, :DK] + tail[:, DK:], got[:, :DK].astype(jnp.float32)


def state_prefix(decay_factor, local_state, axis, reach):
    peers, place = lax.axis_size(axis), lax.axis_index(axis)
    decay, state = send_pair(decay_factor, local_state, axis, 1)
    step = 1
    while step < min(peers, reach):
        earlier_decay, earlier_state = send_pair(decay, state, axis, step)
        state = state + decay[..., None] * earlier_state
        decay = jnp.where(place >= step, decay * earlier_decay, decay)
        step *= 2
    return state


def segments(lengths, packed_order, positions):
    request_count = lengths.shape[0]
    select = (packed_order[:, None] == jnp.arange(request_count, dtype=jnp.int32)[None, :]).astype(
        jnp.int32
    )
    packed_len = jnp.sum(select * lengths[None, :], axis=1)
    end_points = jnp.cumsum(packed_len)
    starts = end_points - packed_len
    segment = jnp.sum((positions[:, None] >= starts[None, :]).astype(jnp.int32), axis=1) - 1
    last_index = jnp.sum(select * (end_points - 1)[:, None], axis=0)
    return (segment, last_index)


def causal_conv(padded, padded_segment, conv_weight, row_count):
    running = jnp.zeros((row_count, padded.shape[1]), jnp.float32)
    current = padded_segment[KCONV - 1 :]
    for offset in range(KCONV):
        window = padded[offset : offset + row_count]
        same_segment = (padded_segment[offset : offset + row_count] == current)[:, None]
        running = running + jnp.where(same_segment, window, 0.0) * conv_weight[offset]
    return running


def activate(convolved, head_count):
    shaped = convolved.reshape(convolved.shape[0], head_count, 2 * DK + DV)
    channel = jnp.arange(2 * DK + DV)
    return jnp.where(channel < 2 * DK, jax.nn.silu(shaped), shaped).astype(jnp.bfloat16)


def head_output(attended, gate_out, head_gain):
    row_count, head_count, value_width = attended.shape
    mean_square = jnp.mean(attended * attended, axis=2, keepdims=True)
    gate_values = jax.nn.silu(
        gate_out.astype(jnp.float32).reshape(row_count, head_count, value_width)
    )
    gated = attended * lax.rsqrt(mean_square + 1e-05) * head_gain * gate_values
    return gated.reshape(row_count, head_count * value_width).astype(jnp.bfloat16)


def shards(
    tokens,
    norm_gain,
    qkv_weight,
    conv_weight,
    gate_down,
    gate_up,
    gate_bias,
    out_gate_weight,
    head_gain,
    out_weight,
    final_gain,
    embedding,
    lengths,
    packed_order,
):
    row_count = tokens.shape[0]
    head_count = out_weight.shape[0] // DV
    tp_size = lax.axis_size("tp")
    tp_index = lax.axis_index("tp")
    column_count = tokens.shape[1] // tp_size
    request_count = lengths.shape[0]
    start_row = lax.axis_index("seq") * row_count
    positions = start_row + jnp.arange(-(KCONV - 1), row_count, dtype=jnp.int32)
    segment_all, last_index = segments(lengths, packed_order, positions)
    segment = segment_all[KCONV - 1 :]
    segment_prior = segment_all[KCONV - 2]
    first_index = last_index - lengths + 1
    residual = tokens.astype(jnp.float32)
    normed = (
        residual
        * lax.rsqrt(jnp.mean(residual * residual, axis=1, keepdims=True) + 1e-06)
        * norm_gain
    ).astype(jnp.bfloat16)
    projected = jnp.dot(normed, qkv_weight, preferred_element_type=jnp.float32).astype(jnp.bfloat16)
    rim_rows = passed_along(projected[row_count - (KCONV - 1) :], "seq", 1)
    padded = jnp.concatenate([rim_rows, projected], axis=0)
    convolved = causal_conv(padded.astype(jnp.float32), segment_all, conv_weight, row_count)
    activated = activate(convolved, head_count)
    lowrank = jnp.dot(normed, gate_down, preferred_element_type=jnp.float32)
    gate_logits = (
        jnp.dot(lowrank, gate_up.astype(jnp.float32), precision=HIGHEST_PRECISION) + gate_bias
    )
    decays = (jax.nn.log_sigmoid(gate_logits) / 16.0).reshape(row_count, head_count, DK)
    gate_out = jnp.dot(normed, out_gate_weight, preferred_element_type=jnp.float32).astype(
        jnp.bfloat16
    )

    offset = last_index - start_row
    owned_here = (offset >= 0) & (offset < row_count)
    edge_list = []
    for tap in range(KCONV - 1):
        located = last_index - (KCONV - 2) + tap
        inside = owned_here & (located >= first_index)
        picked = padded[jnp.clip(located - start_row + KCONV - 1, 0, row_count + KCONV - 2)].astype(
            jnp.float32
        )
        edge_list.append(jnp.where(inside[:, None], picked, 0.0))
    conv_edges = jnp.stack(edge_list, axis=1)

    block_count = row_count // BLOCK
    queries = activated[:, :, :DK].astype(jnp.float32).reshape(block_count, BLOCK, head_count, DK)
    key_rows = activated[:, :, DK : 2 * DK].astype(jnp.float32).reshape(
        block_count, BLOCK, head_count, DK
    )
    values = activated[:, :, 2 * DK :].reshape(block_count, BLOCK, head_count, DV)
    block_segment = segment.reshape(block_count, BLOCK)
    segment_before = segment_all[KCONV - 2 : KCONV - 2 + row_count : BLOCK]
    cumulative = jnp.cumsum(decays.reshape(block_count, BLOCK, head_count, DK), axis=1)
    indices = jnp.arange(BLOCK)
    causal = (indices[None, :] <= indices[:, None])[None] & (
        block_segment[:, None, :] == block_segment[:, :, None]
    )
    allowed = causal[:, :, :, None, None]
    spread = jnp.where(allowed, cumulative[:, :, None] - cumulative[:, None, :], 0.0)
    weights = jnp.where(allowed, jnp.exp(spread), 0.0)
    scores = jnp.sum(queries[:, :, None] * key_rows[:, None, :] * weights, axis=-1).astype(
        jnp.bfloat16
    )
    inside = jnp.einsum("bpqh,bqhv->bphv", scores, values, preferred_element_type=jnp.float32)

    same_tail = (block_segment == block_segment[:, -1:])[:, :, None, None]
    scaled = jnp.where(
        same_tail, key_rows * jnp.exp(cumulative[:, -1:] - cumulative), 0.0
    ).astype(jnp.bfloat16)
    added = jnp.einsum("bjhc,bjhv->bhcv", scaled, values, preferred_element_type=jnp.float32)
    through = block_segment[:, -1] == segment_before
    block_decay = jnp.exp(cumulative[:, -1])
    state = jnp.zeros((head_count, DK, DV), jnp.float32)
    prior = jnp.ones((head_count, DK), jnp.float32)
    states_before, priors = [], []
    for b in range(block_count):
        states_before.append(state)
        priors.append(prior)
        state = jnp.where(through[b], block_decay[b][:, :, None] * state, 0.0) + added[b]
        prior = prior * block_decay[b]
    states_before = jnp.stack(states_before)
    priors = jnp.stack(priors)
    local_state = state
    carried = (block_segment == segment_before[:, None])[:, :, None, None]
    outside = jnp.einsum(
        "bphc,bhcv->bphv", queries * jnp.exp(cumulative), states_before, precision=HIGHEST_PRECISION
    )
    attended = inside + jnp.where(carried, outside, 0.0)

    end_row = jnp.clip(offset, 0, row_count - 1)
    end_block, end_pos = end_row // BLOCK, end_row % BLOCK
    picks = jnp.arange(request_count)
    def at_end_block(array):
        chosen = array[0]
        for b in range(1, block_count):
            hit = (end_block == b).reshape((request_count,) + (1,) * (array.ndim - 1))
            chosen = jnp.where(hit, array[b][None], chosen)
        return chosen

    end_keys_rows = at_end_block(key_rows)
    end_values = at_end_block(values)
    end_cumulative = at_end_block(cumulative)
    end_segments = at_end_block(block_segment)
    end_decay = end_cumulative[picks, end_pos]
    end_segment = end_segments[picks, end_pos]
    end_allowed = (
        (indices[None, :] <= end_pos[:, None]) & (end_segments == end_segment[:, None])
    )[:, :, None, None]
    end_spread = jnp.where(end_allowed, end_decay[:, None] - end_cumulative, 0.0)
    end_weighted = jnp.where(end_allowed, end_keys_rows * jnp.exp(end_spread), 0.0).astype(
        jnp.bfloat16
    )
    within = jnp.einsum("rjhc,rjhv->rhcv", end_weighted, end_values, preferred_element_type=jnp.float32)
    end_carried = (end_segment == at_end_block(segment_before))[:, None, None, None]
    reached = jnp.where(end_carried, jnp.exp(end_decay)[:, :, :, None] * at_end_block(states_before), 0.0)
    local_ends = within + reached

    through_shard = segment[-1] == segment_prior
    decay_factor = jnp.where(through_shard, priors[-1] * block_decay[-1], 0.0)
    incoming = state_prefix(decay_factor, local_state, "seq", -(-MAXLEN // row_count))

    reach = jnp.exp(cumulative) * priors[:, None]
    from_before = (block_segment == segment_prior)[:, :, None, None]
    correction = jnp.einsum(
        "bphc,hcv->bphv",
        jnp.where(from_before, queries * reach, 0.0),
        incoming,
        precision=HIGHEST_PRECISION,
    )
    attended = (attended + correction).reshape(row_count, head_count, DV)
    end_reach = jnp.exp(end_decay) * at_end_block(priors)
    end_from_before = (end_segment == segment_prior)[:, None, None, None]
    end_states = local_ends + jnp.where(
        end_from_before, end_reach[:, :, :, None] * incoming[None], 0.0
    )
    end_states = jnp.where(owned_here[:, None, None, None], end_states, 0.0)
    state_width = head_count * DK * DV
    payload = jnp.concatenate(
        [end_states.reshape(request_count, state_width), conv_edges.reshape(request_count, -1)], axis=1
    )
    payload = lax.psum(payload.astype(jnp.bfloat16), "seq").astype(jnp.float32)
    last_states = payload[:, :state_width].reshape(end_states.shape)
    conv_edges = payload[:, state_width:].reshape(conv_edges.shape)

    gated = head_output(attended, gate_out, head_gain)
    partial = jnp.dot(gated, out_weight, preferred_element_type=jnp.float32).astype(jnp.bfloat16)
    pieces = partial.reshape(row_count, tp_size, column_count)
    arrived = [lax.dynamic_index_in_dim(pieces, tp_index, 1, keepdims=False)]
    for shift in range(1, tp_size):
        outgoing = lax.dynamic_index_in_dim(pieces, (tp_index + shift) % tp_size, 1, keepdims=False)
        arrived.append(
            lax.ppermute(outgoing, "tp", [(i, (i + shift) % tp_size) for i in range(tp_size)])
        )
    arrived = jnp.stack(arrived)
    summed = jnp.zeros((row_count, column_count), jnp.float32)
    for group in range(tp_size):
        summed = summed + lax.dynamic_index_in_dim(
            arrived, (tp_index - group) % tp_size, 0, keepdims=False
        ).astype(jnp.float32)
    column_start = tp_index * column_count
    own_columns = lax.dynamic_slice_in_dim(residual, column_start, column_count, 1)
    hidden = (own_columns + summed).astype(jnp.bfloat16)

    last_rows = jnp.where(owned_here[:, None], hidden[end_row], jnp.zeros((), jnp.bfloat16))
    placed = lax.dynamic_update_slice_in_dim(
        jnp.zeros((request_count, tokens.shape[1]), jnp.bfloat16), last_rows, column_start, 1
    )
    full_rows = butterfly_sum(butterfly_sum(placed, "seq"), "tp").astype(jnp.float32)
    mean_square = jnp.mean(full_rows * full_rows, axis=1)
    last_norms = jnp.sqrt(mean_square)
    final_rows = (full_rows * lax.rsqrt(mean_square[:, None] + 1e-06) * final_gain).astype(
        jnp.bfloat16
    )
    logits = jnp.dot(final_rows, embedding.T, preferred_element_type=jnp.float32)
    max_logits = jnp.max(logits, axis=1, keepdims=True)
    return (hidden, last_states, conv_edges, last_norms, max_logits)


def solution(mesh):
    in_specs = (
        P("seq", None),
        P(),
        P(None, "tp"),
        P(None, "tp"),
        P(),
        P(None, "tp"),
        P("tp"),
        P(None, "tp"),
        P(),
        P("tp", None),
        P(),
        P(("seq", "tp"), None),
        P(),
        P(),
    )
    out_specs = (
        P("seq", "tp"),
        P(None, "tp", None, None),
        P(None, None, "tp"),
        P(),
        P(None, ("seq", "tp")),
    )
    return jax.shard_map(shards, mesh=mesh, in_specs=in_specs, out_specs=out_specs, check_vma=False)
```

```python
import jax
import jax.numpy as jnp
from jax import lax
from jax.sharding import PartitionSpec as P

DK = 256
DV = 512
KCONV = 4
BLOCK = 64
MAXLEN = 4096


HIGHEST_PRECISION = lax.Precision.HIGHEST


def passed_along(array, axis, by):
    peers = lax.axis_size(axis)
    pairs = [(i, i + by) for i in range(peers) if 0 <= i + by < peers]
    return lax.ppermute(array, axis, pairs)


def butterfly_sum(array, axis):
    peers = lax.axis_size(axis)
    step = 1
    while step < peers:
        pairs = [(i, i ^ step) for i in range(peers)]
        array = array + lax.ppermute(array, axis, pairs)
        step *= 2
    return array


def send_pair(decay, state, axis, by):
    high = decay.astype(jnp.bfloat16)
    low = (decay - high.astype(jnp.float32)).astype(jnp.bfloat16)
    row = jnp.concatenate([high, low], axis=-1)[:, None, :]
    packed = jnp.concatenate([state.astype(jnp.bfloat16), row], axis=1)
    got = passed_along(packed, axis, by)
    tail = got[:, DK].astype(jnp.float32)
    return tail[:, :DK] + tail[:, DK:], got[:, :DK].astype(jnp.float32)


def state_prefix(decay_factor, local_state, axis, reach):
    peers, place = lax.axis_size(axis), lax.axis_index(axis)
    decay, state = send_pair(decay_factor, local_state, axis, 1)
    step = 1
    while step < min(peers, reach):
        earlier_decay, earlier_state = send_pair(decay, state, axis, step)
        state = state + decay[..., None] * earlier_state
        decay = jnp.where(place >= step, decay * earlier_decay, decay)
        step *= 2
    return state


def segments(lengths, packed_order, positions):
    request_count = lengths.shape[0]
    select = (packed_order[:, None] == jnp.arange(request_count, dtype=jnp.int32)[None, :]).astype(
        jnp.int32
    )
    packed_len = jnp.sum(select * lengths[None, :], axis=1)
    end_points = jnp.cumsum(packed_len)
    starts = end_points - packed_len
    segment = jnp.sum((positions[:, None] >= starts[None, :]).astype(jnp.int32), axis=1) - 1
    last_index = jnp.sum(select * (end_points - 1)[:, None], axis=0)
    return (segment, last_index)


def causal_conv(padded, padded_segment, conv_weight, row_count):
    running = jnp.zeros((row_count, padded.shape[1]), jnp.float32)
    current = padded_segment[KCONV - 1 :]
    for offset in range(KCONV):
        window = padded[offset : offset + row_count]
        same_segment = (padded_segment[offset : offset + row_count] == current)[:, None]
        running = running + jnp.where(same_segment, window, 0.0) * conv_weight[offset]
    return running


def activate(convolved, head_count):
    shaped = convolved.reshape(convolved.shape[0], head_count, 2 * DK + DV)
    channel = jnp.arange(2 * DK + DV)
    return jnp.where(channel < 2 * DK, jax.nn.silu(shaped), shaped).astype(jnp.bfloat16)


def head_output(attended, gate_out, head_gain):
    row_count, head_count, value_width = attended.shape
    mean_square = jnp.mean(attended * attended, axis=2, keepdims=True)
    gate_values = jax.nn.silu(
        gate_out.astype(jnp.float32).reshape(row_count, head_count, value_width)
    )
    gated = attended * lax.rsqrt(mean_square + 1e-05) * head_gain * gate_values
    return gated.reshape(row_count, head_count * value_width).astype(jnp.bfloat16)


def shards(
    tokens,
    norm_gain,
    qkv_weight,
    conv_weight,
    gate_down,
    gate_up,
    gate_bias,
    out_gate_weight,
    head_gain,
    out_weight,
    final_gain,
    embedding,
    lengths,
    packed_order,
):
    row_count = tokens.shape[0]
    head_count = out_weight.shape[0] // DV
    tp_size = lax.axis_size("tp")
    tp_index = lax.axis_index("tp")
    column_count = tokens.shape[1] // tp_size
    request_count = lengths.shape[0]
    start_row = lax.axis_index("seq") * row_count
    positions = start_row + jnp.arange(-(KCONV - 1), row_count, dtype=jnp.int32)
    segment_all, last_index = segments(lengths, packed_order, positions)
    segment = segment_all[KCONV - 1 :]
    segment_prior = segment_all[KCONV - 2]
    first_index = last_index - lengths + 1
    residual = tokens.astype(jnp.float32)
    normed = (
        residual
        * lax.rsqrt(jnp.mean(residual * residual, axis=1, keepdims=True) + 1e-06)
        * norm_gain
    ).astype(jnp.bfloat16)
    projected = jnp.dot(normed, qkv_weight, preferred_element_type=jnp.float32).astype(jnp.bfloat16)
    rim_rows = passed_along(projected[row_count - (KCONV - 1) :], "seq", 1)
    padded = jnp.concatenate([rim_rows, projected], axis=0)
    convolved = causal_conv(padded.astype(jnp.float32), segment_all, conv_weight, row_count)
    activated = activate(convolved, head_count)
    lowrank = jnp.dot(normed, gate_down, preferred_element_type=jnp.float32)
    gate_logits = (
        jnp.dot(lowrank, gate_up.astype(jnp.float32), precision=HIGHEST_PRECISION) + gate_bias
    )
    decays = (jax.nn.log_sigmoid(gate_logits) / 16.0).reshape(row_count, head_count, DK)
    gate_out = jnp.dot(normed, out_gate_weight, preferred_element_type=jnp.float32).astype(
        jnp.bfloat16
    )

    offset = last_index - start_row
    owned_here = (offset >= 0) & (offset < row_count)
    edge_list = []
    for tap in range(KCONV - 1):
        located = last_index - (KCONV - 2) + tap
        inside = owned_here & (located >= first_index)
        picked = padded[jnp.clip(located - start_row + KCONV - 1, 0, row_count + KCONV - 2)].astype(
            jnp.float32
        )
        edge_list.append(jnp.where(inside[:, None], picked, 0.0))
    conv_edges = jnp.stack(edge_list, axis=1)

    block_count = row_count // BLOCK
    queries = activated[:, :, :DK].astype(jnp.float32).reshape(block_count, BLOCK, head_count, DK)
    key_rows = activated[:, :, DK : 2 * DK].astype(jnp.float32).reshape(
        block_count, BLOCK, head_count, DK
    )
    values = activated[:, :, 2 * DK :].reshape(block_count, BLOCK, head_count, DV)
    block_segment = segment.reshape(block_count, BLOCK)
    segment_before = segment_all[KCONV - 2 : KCONV - 2 + row_count : BLOCK]
    cumulative = jnp.cumsum(decays.reshape(block_count, BLOCK, head_count, DK), axis=1)
    indices = jnp.arange(BLOCK)
    causal = (indices[None, :] <= indices[:, None])[None] & (
        block_segment[:, None, :] == block_segment[:, :, None]
    )
    allowed = causal[:, :, :, None, None]
    spread = jnp.where(allowed, cumulative[:, :, None] - cumulative[:, None, :], 0.0)
    weights = jnp.where(allowed, jnp.exp(spread), 0.0)
    scores = jnp.sum(queries[:, :, None] * key_rows[:, None, :] * weights, axis=-1).astype(
        jnp.bfloat16
    )
    inside = jnp.einsum("bpqh,bqhv->bphv", scores, values, preferred_element_type=jnp.float32)

    same_tail = (block_segment == block_segment[:, -1:])[:, :, None, None]
    scaled = jnp.where(
        same_tail, key_rows * jnp.exp(cumulative[:, -1:] - cumulative), 0.0
    ).astype(jnp.bfloat16)
    added = jnp.einsum("bjhc,bjhv->bhcv", scaled, values, preferred_element_type=jnp.float32)
    through = block_segment[:, -1] == segment_before
    block_decay = jnp.exp(cumulative[:, -1])
    state = jnp.zeros((head_count, DK, DV), jnp.float32)
    prior = jnp.ones((head_count, DK), jnp.float32)
    states_before, priors = [], []
    for b in range(block_count):
        states_before.append(state)
        priors.append(prior)
        state = jnp.where(through[b], block_decay[b][:, :, None] * state, 0.0) + added[b]
        prior = prior * block_decay[b]
    states_before = jnp.stack(states_before)
    priors = jnp.stack(priors)
    local_state = state
    carried = (block_segment == segment_before[:, None])[:, :, None, None]
    outside = jnp.einsum(
        "bphc,bhcv->bphv", queries * jnp.exp(cumulative), states_before, precision=HIGHEST_PRECISION
    )
    attended = inside + jnp.where(carried, outside, 0.0)

    end_row = jnp.clip(offset, 0, row_count - 1)
    end_block, end_pos = end_row // BLOCK, end_row % BLOCK
    picks = jnp.arange(request_count)
    end_keys_rows = key_rows[end_block]
    end_values = values[end_block]
    end_cumulative = cumulative[end_block]
    end_segments = block_segment[end_block]
    end_decay = end_cumulative[picks, end_pos]
    end_segment = end_segments[picks, end_pos]
    end_allowed = (
        (indices[None, :] <= end_pos[:, None]) & (end_segments == end_segment[:, None])
    )[:, :, None, None]
    end_spread = jnp.where(end_allowed, end_decay[:, None] - end_cumulative, 0.0)
    end_weighted = jnp.where(end_allowed, end_keys_rows * jnp.exp(end_spread), 0.0).astype(
        jnp.bfloat16
    )
    within = jnp.einsum("rjhc,rjhv->rhcv", end_weighted, end_values, preferred_element_type=jnp.float32)
    end_carried = (end_segment == segment_before[end_block])[:, None, None, None]
    reached = jnp.where(end_carried, jnp.exp(end_decay)[:, :, :, None] * states_before[end_block], 0.0)
    local_ends = within + reached

    through_shard = segment[-1] == segment_prior
    decay_factor = jnp.where(through_shard, priors[-1] * block_decay[-1], 0.0)
    incoming = state_prefix(decay_factor, local_state, "seq", -(-MAXLEN // row_count))

    reach = jnp.exp(cumulative) * priors[:, None]
    from_before = (block_segment == segment_prior)[:, :, None, None]
    correction = jnp.einsum(
        "bphc,hcv->bphv",
        jnp.where(from_before, queries * reach, 0.0),
        incoming,
        precision=HIGHEST_PRECISION,
    )
    attended = (attended + correction).reshape(row_count, head_count, DV)
    end_reach = jnp.exp(end_decay) * priors[end_block]
    end_from_before = (end_segment == segment_prior)[:, None, None, None]
    end_states = local_ends + jnp.where(
        end_from_before, end_reach[:, :, :, None] * incoming[None], 0.0
    )
    end_states = jnp.where(owned_here[:, None, None, None], end_states, 0.0)
    state_width = head_count * DK * DV
    payload = jnp.concatenate(
        [end_states.reshape(request_count, state_width), conv_edges.reshape(request_count, -1)], axis=1
    )
    payload = lax.psum(payload, "seq")
    last_states = payload[:, :state_width].reshape(end_states.shape)
    conv_edges = payload[:, state_width:].reshape(conv_edges.shape)

    gated = head_output(attended, gate_out, head_gain)
    partial = jnp.dot(gated, out_weight, preferred_element_type=jnp.float32).astype(jnp.bfloat16)
    pieces = partial.reshape(row_count, tp_size, column_count)
    arrived = [lax.dynamic_index_in_dim(pieces, tp_index, 1, keepdims=False)]
    for shift in range(1, tp_size):
        outgoing = lax.dynamic_index_in_dim(pieces, (tp_index + shift) % tp_size, 1, keepdims=False)
        arrived.append(
            lax.ppermute(outgoing, "tp", [(i, (i + shift) % tp_size) for i in range(tp_size)])
        )
    arrived = jnp.stack(arrived)
    summed = jnp.zeros((row_count, column_count), jnp.float32)
    for group in range(tp_size):
        summed = summed + lax.dynamic_index_in_dim(
            arrived, (tp_index - group) % tp_size, 0, keepdims=False
        ).astype(jnp.float32)
    column_start = tp_index * column_count
    own_columns = lax.dynamic_slice_in_dim(residual, column_start, column_count, 1)
    hidden = (own_columns + summed).astype(jnp.bfloat16)

    last_rows = jnp.where(owned_here[:, None], hidden[end_row], jnp.zeros((), jnp.bfloat16))
    placed = lax.dynamic_update_slice_in_dim(
        jnp.zeros((request_count, tokens.shape[1]), jnp.bfloat16), last_rows, column_start, 1
    )
    full_rows = butterfly_sum(butterfly_sum(placed, "seq"), "tp").astype(jnp.float32)
    mean_square = jnp.mean(full_rows * full_rows, axis=1)
    last_norms = jnp.sqrt(mean_square)
    final_rows = (full_rows * lax.rsqrt(mean_square[:, None] + 1e-06) * final_gain).astype(
        jnp.bfloat16
    )
    logits = jnp.dot(final_rows, embedding.T, preferred_element_type=jnp.float32)
    max_logits = jnp.max(logits, axis=1, keepdims=True)
    return (hidden, last_states, conv_edges, last_norms, max_logits)


def solution(mesh):
    in_specs = (
        P("seq", None),
        P(),
        P(None, "tp"),
        P(None, "tp"),
        P(),
        P(None, "tp"),
        P("tp"),
        P(None, "tp"),
        P(),
        P("tp", None),
        P(),
        P(("seq", "tp"), None),
        P(),
        P(),
    )
    out_specs = (
        P("seq", "tp"),
        P(None, "tp", None, None),
        P(None, None, "tp"),
        P(),
        P(None, ("seq", "tp")),
    )
    return jax.shard_map(shards, mesh=mesh, in_specs=in_specs, out_specs=out_specs, check_vma=False)
```

```python
import jax
import jax.numpy as jnp
from jax import lax
from jax.sharding import PartitionSpec as P

DK = 256
DV = 512
KCONV = 4
BLOCK = 64
MAXLEN = 4096


HIGHEST_PRECISION = lax.Precision.HIGHEST


def passed_along(array, axis, by):
    peers = lax.axis_size(axis)
    pairs = [(i, i + by) for i in range(peers) if 0 <= i + by < peers]
    return lax.ppermute(array, axis, pairs)


def butterfly_sum(array, axis):
    peers = lax.axis_size(axis)
    step = 1
    while step < peers:
        pairs = [(i, i ^ step) for i in range(peers)]
        array = array + lax.ppermute(array, axis, pairs)
        step *= 2
    return array


def send_pair(decay, state, axis, by):
    high = decay.astype(jnp.bfloat16)
    low = (decay - high.astype(jnp.float32)).astype(jnp.bfloat16)
    row = jnp.concatenate([high, low], axis=-1)[:, None, :]
    packed = jnp.concatenate([state.astype(jnp.bfloat16), row], axis=1)
    got = passed_along(packed, axis, by)
    tail = got[:, DK].astype(jnp.float32)
    return tail[:, :DK] + tail[:, DK:], got[:, :DK].astype(jnp.float32)


def state_prefix(decay_factor, local_state, axis, reach):
    peers, place = lax.axis_size(axis), lax.axis_index(axis)
    decay, state = send_pair(decay_factor, local_state, axis, 1)
    step = 1
    while step < min(peers, reach):
        earlier_decay, earlier_state = send_pair(decay, state, axis, step)
        state = state + decay[..., None] * earlier_state
        decay = jnp.where(place >= step, decay * earlier_decay, decay)
        step *= 2
    return state


def segments(lengths, packed_order, positions):
    request_count = lengths.shape[0]
    select = (packed_order[:, None] == jnp.arange(request_count, dtype=jnp.int32)[None, :]).astype(
        jnp.int32
    )
    packed_len = jnp.sum(select * lengths[None, :], axis=1)
    end_points = jnp.cumsum(packed_len)
    starts = end_points - packed_len
    segment = jnp.sum((positions[:, None] >= starts[None, :]).astype(jnp.int32), axis=1) - 1
    last_index = jnp.sum(select * (end_points - 1)[:, None], axis=0)
    return (segment, last_index)


def causal_conv(padded, padded_segment, conv_weight, row_count):
    running = jnp.zeros((row_count, padded.shape[1]), jnp.float32)
    current = padded_segment[KCONV - 1 :]
    for offset in range(KCONV):
        window = padded[offset : offset + row_count]
        same_segment = (padded_segment[offset : offset + row_count] == current)[:, None]
        running = running + jnp.where(same_segment, window, 0.0) * conv_weight[offset]
    return running


def activate(convolved, head_count):
    shaped = convolved.reshape(convolved.shape[0], head_count, 2 * DK + DV)
    channel = jnp.arange(2 * DK + DV)
    return jnp.where(channel < 2 * DK, jax.nn.silu(shaped), shaped).astype(jnp.bfloat16)


def head_output(attended, gate_out, head_gain):
    row_count, head_count, value_width = attended.shape
    mean_square = jnp.mean(attended * attended, axis=2, keepdims=True)
    gate_values = jax.nn.silu(
        gate_out.astype(jnp.float32).reshape(row_count, head_count, value_width)
    )
    gated = attended * lax.rsqrt(mean_square + 1e-05) * head_gain * gate_values
    return gated.reshape(row_count, head_count * value_width).astype(jnp.bfloat16)


def shards(
    tokens,
    norm_gain,
    qkv_weight,
    conv_weight,
    gate_down,
    gate_up,
    gate_bias,
    out_gate_weight,
    head_gain,
    out_weight,
    final_gain,
    embedding,
    lengths,
    packed_order,
):
    row_count = tokens.shape[0]
    head_count = out_weight.shape[0] // DV
    tp_size = lax.axis_size("tp")
    tp_index = lax.axis_index("tp")
    column_count = tokens.shape[1] // tp_size
    request_count = lengths.shape[0]
    start_row = lax.axis_index("seq") * row_count
    positions = start_row + jnp.arange(-(KCONV - 1), row_count, dtype=jnp.int32)
    segment_all, last_index = segments(lengths, packed_order, positions)
    segment = segment_all[KCONV - 1 :]
    segment_prior = segment_all[KCONV - 2]
    first_index = last_index - lengths + 1
    residual = tokens.astype(jnp.float32)
    normed = (
        residual
        * lax.rsqrt(jnp.mean(residual * residual, axis=1, keepdims=True) + 1e-06)
        * norm_gain
    ).astype(jnp.bfloat16)
    projected = jnp.dot(normed, qkv_weight, preferred_element_type=jnp.float32).astype(jnp.bfloat16)
    rim_rows = passed_along(projected[row_count - (KCONV - 1) :], "seq", 1)
    padded = jnp.concatenate([rim_rows, projected], axis=0)
    convolved = causal_conv(padded.astype(jnp.float32), segment_all, conv_weight, row_count)
    activated = activate(convolved, head_count)
    lowrank = jnp.dot(normed, gate_down, preferred_element_type=jnp.float32)
    gate_logits = (
        jnp.dot(lowrank, gate_up.astype(jnp.float32), precision=HIGHEST_PRECISION) + gate_bias
    )
    decays = (jax.nn.log_sigmoid(gate_logits) / 16.0).reshape(row_count, head_count, DK)
    gate_out = jnp.dot(normed, out_gate_weight, preferred_element_type=jnp.float32).astype(
        jnp.bfloat16
    )

    offset = last_index - start_row
    owned_here = (offset >= 0) & (offset < row_count)
    edge_list = []
    for tap in range(KCONV - 1):
        located = last_index - (KCONV - 2) + tap
        inside = owned_here & (located >= first_index)
        picked = padded[jnp.clip(located - start_row + KCONV - 1, 0, row_count + KCONV - 2)].astype(
            jnp.float32
        )
        edge_list.append(jnp.where(inside[:, None], picked, 0.0))
    conv_edges = jnp.stack(edge_list, axis=1)

    block_count = row_count // BLOCK
    queries = activated[:, :, :DK].astype(jnp.float32).reshape(block_count, BLOCK, head_count, DK)
    key_rows = activated[:, :, DK : 2 * DK].astype(jnp.float32).reshape(
        block_count, BLOCK, head_count, DK
    )
    values = activated[:, :, 2 * DK :].reshape(block_count, BLOCK, head_count, DV)
    block_segment = segment.reshape(block_count, BLOCK)
    segment_before = segment_all[KCONV - 2 : KCONV - 2 + row_count : BLOCK]
    cumulative = jnp.cumsum(decays.reshape(block_count, BLOCK, head_count, DK), axis=1)
    indices = jnp.arange(BLOCK)
    causal = (indices[None, :] <= indices[:, None])[None] & (
        block_segment[:, None, :] == block_segment[:, :, None]
    )
    allowed = causal[:, :, :, None, None]
    spread = jnp.where(allowed, cumulative[:, :, None] - cumulative[:, None, :], 0.0)
    weights = jnp.where(allowed, jnp.exp(spread), 0.0)
    scores = jnp.sum(queries[:, :, None] * key_rows[:, None, :] * weights, axis=-1).astype(
        jnp.bfloat16
    )
    inside = jnp.einsum("bpqh,bqhv->bphv", scores, values, preferred_element_type=jnp.float32)

    same_tail = (block_segment == block_segment[:, -1:])[:, :, None, None]
    scaled = jnp.where(
        same_tail, key_rows * jnp.exp(cumulative[:, -1:] - cumulative), 0.0
    ).astype(jnp.bfloat16)
    added = jnp.einsum("bjhc,bjhv->bhcv", scaled, values, preferred_element_type=jnp.float32)
    through = block_segment[:, -1] == segment_before
    block_decay = jnp.exp(cumulative[:, -1])
    state = jnp.zeros((head_count, DK, DV), jnp.float32)
    prior = jnp.ones((head_count, DK), jnp.float32)
    states_before, priors = [], []
    for b in range(block_count):
        states_before.append(state)
        priors.append(prior)
        state = jnp.where(through[b], block_decay[b][:, :, None] * state, 0.0) + added[b]
        prior = prior * block_decay[b]
    states_before = jnp.stack(states_before)
    priors = jnp.stack(priors)
    local_state = state
    carried = (block_segment == segment_before[:, None])[:, :, None, None]
    outside = jnp.einsum(
        "bphc,bhcv->bphv", queries * jnp.exp(cumulative), states_before, precision=HIGHEST_PRECISION
    )
    attended = inside + jnp.where(carried, outside, 0.0)

    end_row = jnp.clip(offset, 0, row_count - 1)
    end_block, end_pos = end_row // BLOCK, end_row % BLOCK
    picks = jnp.arange(request_count)
    end_keys_rows = key_rows[end_block]
    end_values = values[end_block]
    end_cumulative = cumulative[end_block]
    end_segments = block_segment[end_block]
    end_decay = end_cumulative[picks, end_pos]
    end_segment = end_segments[picks, end_pos]
    end_allowed = (
        (indices[None, :] <= end_pos[:, None]) & (end_segments == end_segment[:, None])
    )[:, :, None, None]
    end_spread = jnp.where(end_allowed, end_decay[:, None] - end_cumulative, 0.0)
    end_weighted = jnp.where(end_allowed, end_keys_rows * jnp.exp(end_spread), 0.0).astype(
        jnp.bfloat16
    )
    within = jnp.einsum("rjhc,rjhv->rhcv", end_weighted, end_values, preferred_element_type=jnp.float32)
    end_carried = (end_segment == segment_before[end_block])[:, None, None, None]
    reached = jnp.where(end_carried, jnp.exp(end_decay)[:, :, :, None] * states_before[end_block], 0.0)
    local_ends = within + reached

    seq_size, seq_index = lax.axis_size("seq"), lax.axis_index("seq")
    through_shard = segment[-1] == segment_prior
    decay_factor = jnp.where(through_shard, priors[-1] * block_decay[-1], 0.0)
    end_reach = jnp.exp(end_decay) * priors[end_block]
    end_from_before = end_segment == segment_prior
    reach_here = jnp.where((owned_here & end_from_before)[:, None, None], end_reach, 0.0)
    table = jnp.concatenate(
        [
            jnp.where((jnp.arange(seq_size) == seq_index)[:, None, None], decay_factor[None], 0.0),
            reach_here,
        ]
    )
    table = butterfly_sum(table, "seq")
    shard_decays, end_reaches = table[:seq_size], table[seq_size:]
    end_shard = last_index // row_count
    shard_ids = jnp.arange(seq_size)
    between = (shard_ids[None, :] > seq_index) & (shard_ids[None, :] < end_shard[:, None])
    spanned = jnp.prod(jnp.where(between[:, :, None, None], shard_decays[None], 1.0), axis=1)
    from_here = (seq_index < end_shard)[:, None, None, None]
    end_terms = jnp.where(owned_here[:, None, None, None], local_ends, 0.0) + jnp.where(
        from_here, (end_reaches * spanned)[:, :, :, None] * local_state[None], 0.0
    )
    state_width = head_count * DK * DV
    payload = jnp.concatenate(
        [end_terms.reshape(request_count, state_width), conv_edges.reshape(request_count, -1)], axis=1
    )
    payload = lax.psum(payload, "seq")
    last_states = payload[:, :state_width].reshape(local_ends.shape)
    conv_edges = payload[:, state_width:].reshape(conv_edges.shape)

    incoming = state_prefix(decay_factor, local_state, "seq", -(-MAXLEN // row_count))
    reach = jnp.exp(cumulative) * priors[:, None]
    from_before = (block_segment == segment_prior)[:, :, None, None]
    correction = jnp.einsum(
        "bphc,hcv->bphv",
        jnp.where(from_before, queries * reach, 0.0),
        incoming,
        precision=HIGHEST_PRECISION,
    )
    attended = (attended + correction).reshape(row_count, head_count, DV)

    gated = head_output(attended, gate_out, head_gain)
    partial = jnp.dot(gated, out_weight, preferred_element_type=jnp.float32).astype(jnp.bfloat16)
    pieces = partial.reshape(row_count, tp_size, column_count)
    arrived = [lax.dynamic_index_in_dim(pieces, tp_index, 1, keepdims=False)]
    for shift in range(1, tp_size):
        outgoing = lax.dynamic_index_in_dim(pieces, (tp_index + shift) % tp_size, 1, keepdims=False)
        arrived.append(
            lax.ppermute(outgoing, "tp", [(i, (i + shift) % tp_size) for i in range(tp_size)])
        )
    arrived = jnp.stack(arrived)
    summed = jnp.zeros((row_count, column_count), jnp.float32)
    for group in range(tp_size):
        summed = summed + lax.dynamic_index_in_dim(
            arrived, (tp_index - group) % tp_size, 0, keepdims=False
        ).astype(jnp.float32)
    column_start = tp_index * column_count
    own_columns = lax.dynamic_slice_in_dim(residual, column_start, column_count, 1)
    hidden = (own_columns + summed).astype(jnp.bfloat16)

    last_rows = jnp.where(owned_here[:, None], hidden[end_row], jnp.zeros((), jnp.bfloat16))
    placed = lax.dynamic_update_slice_in_dim(
        jnp.zeros((request_count, tokens.shape[1]), jnp.bfloat16), last_rows, column_start, 1
    )
    full_rows = butterfly_sum(butterfly_sum(placed, "seq"), "tp").astype(jnp.float32)
    mean_square = jnp.mean(full_rows * full_rows, axis=1)
    last_norms = jnp.sqrt(mean_square)
    final_rows = (full_rows * lax.rsqrt(mean_square[:, None] + 1e-06) * final_gain).astype(
        jnp.bfloat16
    )
    logits = jnp.dot(final_rows, embedding.T, preferred_element_type=jnp.float32)
    max_logits = jnp.max(logits, axis=1, keepdims=True)
    return (hidden, last_states, conv_edges, last_norms, max_logits)


def solution(mesh):
    in_specs = (
        P("seq", None),
        P(),
        P(None, "tp"),
        P(None, "tp"),
        P(),
        P(None, "tp"),
        P("tp"),
        P(None, "tp"),
        P(),
        P("tp", None),
        P(),
        P(("seq", "tp"), None),
        P(),
        P(),
    )
    out_specs = (
        P("seq", "tp"),
        P(None, "tp", None, None),
        P(None, None, "tp"),
        P(),
        P(None, ("seq", "tp")),
    )
    return jax.shard_map(shards, mesh=mesh, in_specs=in_specs, out_specs=out_specs, check_vma=False)
```

```python
import jax
import jax.numpy as jnp
from jax import lax
from jax.sharding import PartitionSpec as P

DK = 256
DV = 512
KCONV = 4
BLOCK = 64
MAXLEN = 4096


HIGHEST_PRECISION = lax.Precision.HIGHEST


def passed_along(array, axis, by):
    peers = lax.axis_size(axis)
    pairs = [(i, i + by) for i in range(peers) if 0 <= i + by < peers]
    return lax.ppermute(array, axis, pairs)


def butterfly_sum(array, axis):
    peers = lax.axis_size(axis)
    step = 1
    while step < peers:
        pairs = [(i, i ^ step) for i in range(peers)]
        array = array + lax.ppermute(array, axis, pairs)
        step *= 2
    return array


def send_pair(decay, state, axis, by):
    high = decay.astype(jnp.bfloat16)
    low = (decay - high.astype(jnp.float32)).astype(jnp.bfloat16)
    row = jnp.concatenate([high, low], axis=-1)[:, None, :]
    packed = jnp.concatenate([state.astype(jnp.bfloat16), row], axis=1)
    got = passed_along(packed, axis, by)
    tail = got[:, DK].astype(jnp.float32)
    return tail[:, :DK] + tail[:, DK:], got[:, :DK].astype(jnp.float32)


def state_prefix(decay_factor, local_state, axis, reach):
    peers, place = lax.axis_size(axis), lax.axis_index(axis)
    decay, state = send_pair(decay_factor, local_state, axis, 1)
    step = 1
    while step < min(peers, reach):
        earlier_decay, earlier_state = send_pair(decay, state, axis, step)
        state = state + decay[..., None] * earlier_state
        decay = jnp.where(place >= step, decay * earlier_decay, decay)
        step *= 2
    return state


def segments(lengths, packed_order, positions):
    request_count = lengths.shape[0]
    select = (packed_order[:, None] == jnp.arange(request_count, dtype=jnp.int32)[None, :]).astype(
        jnp.int32
    )
    packed_len = jnp.sum(select * lengths[None, :], axis=1)
    end_points = jnp.cumsum(packed_len)
    starts = end_points - packed_len
    segment = jnp.sum((positions[:, None] >= starts[None, :]).astype(jnp.int32), axis=1) - 1
    last_index = jnp.sum(select * (end_points - 1)[:, None], axis=0)
    return (segment, last_index)


def causal_conv(padded, padded_segment, conv_weight, row_count):
    running = jnp.zeros((row_count, padded.shape[1]), jnp.float32)
    current = padded_segment[KCONV - 1 :]
    for offset in range(KCONV):
        window = padded[offset : offset + row_count]
        same_segment = (padded_segment[offset : offset + row_count] == current)[:, None]
        running = running + jnp.where(same_segment, window, 0.0) * conv_weight[offset]
    return running


def activate(convolved, head_count):
    shaped = convolved.reshape(convolved.shape[0], head_count, 2 * DK + DV)
    channel = jnp.arange(2 * DK + DV)
    return jnp.where(channel < 2 * DK, jax.nn.silu(shaped), shaped).astype(jnp.bfloat16)


def head_output(attended, gate_out, head_gain):
    row_count, head_count, value_width = attended.shape
    mean_square = jnp.mean(attended * attended, axis=2, keepdims=True)
    gate_values = jax.nn.silu(
        gate_out.astype(jnp.float32).reshape(row_count, head_count, value_width)
    )
    gated = attended * lax.rsqrt(mean_square + 1e-05) * head_gain * gate_values
    return gated.reshape(row_count, head_count * value_width).astype(jnp.bfloat16)


def shards(
    tokens,
    norm_gain,
    qkv_weight,
    conv_weight,
    gate_down,
    gate_up,
    gate_bias,
    out_gate_weight,
    head_gain,
    out_weight,
    final_gain,
    embedding,
    lengths,
    packed_order,
):
    row_count = tokens.shape[0]
    head_count = out_weight.shape[0] // DV
    tp_size = lax.axis_size("tp")
    tp_index = lax.axis_index("tp")
    column_count = tokens.shape[1] // tp_size
    request_count = lengths.shape[0]
    start_row = lax.axis_index("seq") * row_count
    positions = start_row + jnp.arange(-(KCONV - 1), row_count, dtype=jnp.int32)
    segment_all, last_index = segments(lengths, packed_order, positions)
    segment = segment_all[KCONV - 1 :]
    segment_prior = segment_all[KCONV - 2]
    first_index = last_index - lengths + 1
    residual = tokens.astype(jnp.float32)
    normed = (
        residual
        * lax.rsqrt(jnp.mean(residual * residual, axis=1, keepdims=True) + 1e-06)
        * norm_gain
    ).astype(jnp.bfloat16)
    projected = jnp.dot(normed, qkv_weight, preferred_element_type=jnp.float32).astype(jnp.bfloat16)
    rim_rows = passed_along(projected[row_count - (KCONV - 1) :], "seq", 1)
    padded = jnp.concatenate([rim_rows, projected], axis=0)
    convolved = causal_conv(padded.astype(jnp.float32), segment_all, conv_weight, row_count)
    activated = activate(convolved, head_count)
    lowrank = jnp.dot(normed, gate_down, preferred_element_type=jnp.float32)
    gate_logits = (
        jnp.dot(lowrank, gate_up.astype(jnp.float32), precision=HIGHEST_PRECISION) + gate_bias
    )
    decays = (jax.nn.log_sigmoid(gate_logits) / 16.0).reshape(row_count, head_count, DK)
    gate_out = jnp.dot(normed, out_gate_weight, preferred_element_type=jnp.float32).astype(
        jnp.bfloat16
    )

    offset = last_index - start_row
    owned_here = (offset >= 0) & (offset < row_count)
    edge_list = []
    for tap in range(KCONV - 1):
        located = last_index - (KCONV - 2) + tap
        inside = owned_here & (located >= first_index)
        picked = padded[jnp.clip(located - start_row + KCONV - 1, 0, row_count + KCONV - 2)].astype(
            jnp.float32
        )
        edge_list.append(jnp.where(inside[:, None], picked, 0.0))
    conv_edges = jnp.stack(edge_list, axis=1)

    block_count = row_count // BLOCK
    queries = activated[:, :, :DK].astype(jnp.float32).reshape(block_count, BLOCK, head_count, DK)
    key_rows = activated[:, :, DK : 2 * DK].astype(jnp.float32).reshape(
        block_count, BLOCK, head_count, DK
    )
    values = activated[:, :, 2 * DK :].reshape(block_count, BLOCK, head_count, DV)
    block_segment = segment.reshape(block_count, BLOCK)
    segment_before = segment_all[KCONV - 2 : KCONV - 2 + row_count : BLOCK]
    cumulative = jnp.cumsum(decays.reshape(block_count, BLOCK, head_count, DK), axis=1)
    indices = jnp.arange(BLOCK)
    causal = (indices[None, :] <= indices[:, None])[None] & (
        block_segment[:, None, :] == block_segment[:, :, None]
    )
    allowed = causal[:, :, :, None, None]
    spread = jnp.where(allowed, cumulative[:, :, None] - cumulative[:, None, :], 0.0)
    weights = jnp.where(allowed, jnp.exp(spread), 0.0)
    scores = jnp.sum(queries[:, :, None] * key_rows[:, None, :] * weights, axis=-1).astype(
        jnp.bfloat16
    )
    inside = jnp.einsum("bpqh,bqhv->bphv", scores, values, preferred_element_type=jnp.float32)

    same_tail = (block_segment == block_segment[:, -1:])[:, :, None, None]
    scaled = jnp.where(
        same_tail, key_rows * jnp.exp(cumulative[:, -1:] - cumulative), 0.0
    ).astype(jnp.bfloat16)
    added = jnp.einsum("bjhc,bjhv->bhcv", scaled, values, preferred_element_type=jnp.float32)
    through = block_segment[:, -1] == segment_before
    block_decay = jnp.exp(cumulative[:, -1])
    state = jnp.zeros((head_count, DK, DV), jnp.float32)
    prior = jnp.ones((head_count, DK), jnp.float32)
    states_before, priors = [], []
    for b in range(block_count):
        states_before.append(state)
        priors.append(prior)
        state = jnp.where(through[b], block_decay[b][:, :, None] * state, 0.0) + added[b]
        prior = prior * block_decay[b]
    states_before = jnp.stack(states_before)
    priors = jnp.stack(priors)
    local_state = state
    carried = (block_segment == segment_before[:, None])[:, :, None, None]
    outside = jnp.einsum(
        "bphc,bhcv->bphv", queries * jnp.exp(cumulative), states_before, precision=HIGHEST_PRECISION
    )
    attended = inside + jnp.where(carried, outside, 0.0)

    end_row = jnp.clip(offset, 0, row_count - 1)
    end_block, end_pos = end_row // BLOCK, end_row % BLOCK
    picks = jnp.arange(request_count)
    def at_end_block(array):
        chosen = array[0]
        for b in range(1, block_count):
            hit = (end_block == b).reshape((request_count,) + (1,) * (array.ndim - 1))
            chosen = jnp.where(hit, array[b][None], chosen)
        return chosen

    end_keys_rows = at_end_block(key_rows)
    end_values = at_end_block(values)
    end_cumulative = at_end_block(cumulative)
    end_segments = at_end_block(block_segment)
    end_decay = end_cumulative[picks, end_pos]
    end_segment = end_segments[picks, end_pos]
    end_allowed = (
        (indices[None, :] <= end_pos[:, None]) & (end_segments == end_segment[:, None])
    )[:, :, None, None]
    end_spread = jnp.where(end_allowed, end_decay[:, None] - end_cumulative, 0.0)
    end_weighted = jnp.where(end_allowed, end_keys_rows * jnp.exp(end_spread), 0.0).astype(
        jnp.bfloat16
    )
    within = jnp.einsum("rjhc,rjhv->rhcv", end_weighted, end_values, preferred_element_type=jnp.float32)
    end_carried = (end_segment == at_end_block(segment_before))[:, None, None, None]
    reached = jnp.where(end_carried, jnp.exp(end_decay)[:, :, :, None] * at_end_block(states_before), 0.0)
    local_ends = within + reached

    through_shard = segment[-1] == segment_prior
    decay_factor = jnp.where(through_shard, priors[-1] * block_decay[-1], 0.0)
    incoming = state_prefix(decay_factor, local_state, "seq", -(-MAXLEN // row_count))

    reach = jnp.exp(cumulative) * priors[:, None]
    from_before = (block_segment == segment_prior)[:, :, None, None]
    correction = jnp.einsum(
        "bphc,hcv->bphv",
        jnp.where(from_before, queries * reach, 0.0),
        incoming,
        precision=HIGHEST_PRECISION,
    )
    attended = (attended + correction).reshape(row_count, head_count, DV)
    end_reach = jnp.exp(end_decay) * at_end_block(priors)
    end_from_before = (end_segment == segment_prior)[:, None, None, None]
    end_states = local_ends + jnp.where(
        end_from_before, end_reach[:, :, :, None] * incoming[None], 0.0
    )
    end_states = jnp.where(owned_here[:, None, None, None], end_states, 0.0)
    edge_rows = conv_edges.reshape(request_count, head_count, -1, DV)
    payload = lax.psum(jnp.concatenate([end_states, edge_rows], axis=2), "seq")
    last_states = payload[:, :, :DK]
    conv_edges = payload[:, :, DK:].reshape(conv_edges.shape)

    gated = head_output(attended, gate_out, head_gain)
    partial = jnp.dot(gated, out_weight, preferred_element_type=jnp.float32).astype(jnp.bfloat16)
    pieces = partial.reshape(row_count, tp_size, column_count)
    arrived = [lax.dynamic_index_in_dim(pieces, tp_index, 1, keepdims=False)]
    for shift in range(1, tp_size):
        outgoing = lax.dynamic_index_in_dim(pieces, (tp_index + shift) % tp_size, 1, keepdims=False)
        arrived.append(
            lax.ppermute(outgoing, "tp", [(i, (i + shift) % tp_size) for i in range(tp_size)])
        )
    arrived = jnp.stack(arrived)
    summed = jnp.zeros((row_count, column_count), jnp.float32)
    for group in range(tp_size):
        summed = summed + lax.dynamic_index_in_dim(
            arrived, (tp_index - group) % tp_size, 0, keepdims=False
        ).astype(jnp.float32)
    column_start = tp_index * column_count
    own_columns = lax.dynamic_slice_in_dim(residual, column_start, column_count, 1)
    hidden = (own_columns + summed).astype(jnp.bfloat16)

    last_rows = jnp.where(owned_here[:, None], hidden[end_row], jnp.zeros((), jnp.bfloat16))
    placed = lax.dynamic_update_slice_in_dim(
        jnp.zeros((request_count, tokens.shape[1]), jnp.bfloat16), last_rows, column_start, 1
    )
    full_rows = butterfly_sum(butterfly_sum(placed, "seq"), "tp").astype(jnp.float32)
    mean_square = jnp.mean(full_rows * full_rows, axis=1)
    last_norms = jnp.sqrt(mean_square)
    final_rows = (full_rows * lax.rsqrt(mean_square[:, None] + 1e-06) * final_gain).astype(
        jnp.bfloat16
    )
    logits = jnp.dot(final_rows, embedding.T, preferred_element_type=jnp.float32)
    max_logits = jnp.max(logits, axis=1, keepdims=True)
    return (hidden, last_states, conv_edges, last_norms, max_logits)


def solution(mesh):
    in_specs = (
        P("seq", None),
        P(),
        P(None, "tp"),
        P(None, "tp"),
        P(),
        P(None, "tp"),
        P("tp"),
        P(None, "tp"),
        P(),
        P("tp", None),
        P(),
        P(("seq", "tp"), None),
        P(),
        P(),
    )
    out_specs = (
        P("seq", "tp"),
        P(None, "tp", None, None),
        P(None, None, "tp"),
        P(),
        P(None, ("seq", "tp")),
    )
    return jax.shard_map(shards, mesh=mesh, in_specs=in_specs, out_specs=out_specs, check_vma=False)
```

```python
import jax
import jax.numpy as jnp
from jax import lax
from jax.sharding import PartitionSpec as P

DK = 256
DV = 512
KCONV = 4
BLOCK = 64
MAXLEN = 4096


HIGHEST_PRECISION = lax.Precision.HIGHEST


def passed_along(array, axis, by):
    peers = lax.axis_size(axis)
    pairs = [(i, i + by) for i in range(peers) if 0 <= i + by < peers]
    return lax.ppermute(array, axis, pairs)


def butterfly_sum(array, axis):
    peers = lax.axis_size(axis)
    step = 1
    while step < peers:
        pairs = [(i, i ^ step) for i in range(peers)]
        array = array + lax.ppermute(array, axis, pairs)
        step *= 2
    return array


def send_pair(decay, state, axis, by):
    high = decay.astype(jnp.bfloat16)
    low = (decay - high.astype(jnp.float32)).astype(jnp.bfloat16)
    row = jnp.concatenate([high, low], axis=-1)[:, None, :]
    packed = jnp.concatenate([state.astype(jnp.bfloat16), row], axis=1)
    got = passed_along(packed, axis, by)
    tail = got[:, DK].astype(jnp.float32)
    return tail[:, :DK] + tail[:, DK:], got[:, :DK].astype(jnp.float32)


def state_prefix(decay_factor, local_state, axis, reach):
    peers = lax.axis_size(axis)
    limit = min(peers, reach)
    decay, state = send_pair(decay_factor, local_state, axis, 1)
    step = 1
    while step < limit:
        radix = min(4, -(-limit // step))
        earlier = [send_pair(decay, state, axis, k * step) for k in range(1, radix)]
        for earlier_decay, earlier_state in earlier:
            state = state + decay[..., None] * earlier_state
            decay = decay * earlier_decay
        step *= radix
    return state


def segments(lengths, packed_order, positions):
    request_count = lengths.shape[0]
    select = (packed_order[:, None] == jnp.arange(request_count, dtype=jnp.int32)[None, :]).astype(
        jnp.int32
    )
    packed_len = jnp.sum(select * lengths[None, :], axis=1)
    end_points = jnp.cumsum(packed_len)
    starts = end_points - packed_len
    segment = jnp.sum((positions[:, None] >= starts[None, :]).astype(jnp.int32), axis=1) - 1
    last_index = jnp.sum(select * (end_points - 1)[:, None], axis=0)
    return (segment, last_index)


def causal_conv(padded, padded_segment, conv_weight, row_count):
    running = jnp.zeros((row_count, padded.shape[1]), jnp.float32)
    current = padded_segment[KCONV - 1 :]
    for offset in range(KCONV):
        window = padded[offset : offset + row_count]
        same_segment = (padded_segment[offset : offset + row_count] == current)[:, None]
        running = running + jnp.where(same_segment, window, 0.0) * conv_weight[offset]
    return running


def activate(convolved, head_count):
    shaped = convolved.reshape(convolved.shape[0], head_count, 2 * DK + DV)
    channel = jnp.arange(2 * DK + DV)
    return jnp.where(channel < 2 * DK, jax.nn.silu(shaped), shaped).astype(jnp.bfloat16)


def head_output(attended, gate_out, head_gain):
    row_count, head_count, value_width = attended.shape
    mean_square = jnp.mean(attended * attended, axis=2, keepdims=True)
    gate_values = jax.nn.silu(
        gate_out.astype(jnp.float32).reshape(row_count, head_count, value_width)
    )
    gated = attended * lax.rsqrt(mean_square + 1e-05) * head_gain * gate_values
    return gated.reshape(row_count, head_count * value_width).astype(jnp.bfloat16)


def shards(
    tokens,
    norm_gain,
    qkv_weight,
    conv_weight,
    gate_down,
    gate_up,
    gate_bias,
    out_gate_weight,
    head_gain,
    out_weight,
    final_gain,
    embedding,
    lengths,
    packed_order,
):
    row_count = tokens.shape[0]
    head_count = out_weight.shape[0] // DV
    tp_size = lax.axis_size("tp")
    tp_index = lax.axis_index("tp")
    column_count = tokens.shape[1] // tp_size
    request_count = lengths.shape[0]
    start_row = lax.axis_index("seq") * row_count
    positions = start_row + jnp.arange(-(KCONV - 1), row_count, dtype=jnp.int32)
    segment_all, last_index = segments(lengths, packed_order, positions)
    segment = segment_all[KCONV - 1 :]
    segment_prior = segment_all[KCONV - 2]
    first_index = last_index - lengths + 1
    residual = tokens.astype(jnp.float32)
    normed = (
        residual
        * lax.rsqrt(jnp.mean(residual * residual, axis=1, keepdims=True) + 1e-06)
        * norm_gain
    ).astype(jnp.bfloat16)
    projected = jnp.dot(normed, qkv_weight, preferred_element_type=jnp.float32).astype(jnp.bfloat16)
    rim_rows = passed_along(projected[row_count - (KCONV - 1) :], "seq", 1)
    padded = jnp.concatenate([rim_rows, projected], axis=0)
    convolved = causal_conv(padded.astype(jnp.float32), segment_all, conv_weight, row_count)
    activated = activate(convolved, head_count)
    lowrank = jnp.dot(normed, gate_down, preferred_element_type=jnp.float32)
    gate_logits = (
        jnp.dot(lowrank, gate_up.astype(jnp.float32), precision=HIGHEST_PRECISION) + gate_bias
    )
    decays = (jax.nn.log_sigmoid(gate_logits) / 16.0).reshape(row_count, head_count, DK)
    gate_out = jnp.dot(normed, out_gate_weight, preferred_element_type=jnp.float32).astype(
        jnp.bfloat16
    )

    offset = last_index - start_row
    owned_here = (offset >= 0) & (offset < row_count)
    edge_list = []
    for tap in range(KCONV - 1):
        located = last_index - (KCONV - 2) + tap
        inside = owned_here & (located >= first_index)
        picked = padded[jnp.clip(located - start_row + KCONV - 1, 0, row_count + KCONV - 2)].astype(
            jnp.float32
        )
        edge_list.append(jnp.where(inside[:, None], picked, 0.0))
    conv_edges = jnp.stack(edge_list, axis=1)

    block_count = row_count // BLOCK
    queries = activated[:, :, :DK].astype(jnp.float32).reshape(block_count, BLOCK, head_count, DK)
    key_rows = activated[:, :, DK : 2 * DK].astype(jnp.float32).reshape(
        block_count, BLOCK, head_count, DK
    )
    values = activated[:, :, 2 * DK :].reshape(block_count, BLOCK, head_count, DV)
    block_segment = segment.reshape(block_count, BLOCK)
    segment_before = segment_all[KCONV - 2 : KCONV - 2 + row_count : BLOCK]
    cumulative = jnp.cumsum(decays.reshape(block_count, BLOCK, head_count, DK), axis=1)
    indices = jnp.arange(BLOCK)
    causal = (indices[None, :] <= indices[:, None])[None] & (
        block_segment[:, None, :] == block_segment[:, :, None]
    )
    allowed = causal[:, :, :, None, None]
    spread = jnp.where(allowed, cumulative[:, :, None] - cumulative[:, None, :], 0.0)
    weights = jnp.where(allowed, jnp.exp(spread), 0.0)
    scores = jnp.sum(queries[:, :, None] * key_rows[:, None, :] * weights, axis=-1).astype(
        jnp.bfloat16
    )
    inside = jnp.einsum("bpqh,bqhv->bphv", scores, values, preferred_element_type=jnp.float32)

    same_tail = (block_segment == block_segment[:, -1:])[:, :, None, None]
    scaled = jnp.where(
        same_tail, key_rows * jnp.exp(cumulative[:, -1:] - cumulative), 0.0
    ).astype(jnp.bfloat16)
    added = jnp.einsum("bjhc,bjhv->bhcv", scaled, values, preferred_element_type=jnp.float32)
    through = block_segment[:, -1] == segment_before
    block_decay = jnp.exp(cumulative[:, -1])
    state = jnp.zeros((head_count, DK, DV), jnp.float32)
    prior = jnp.ones((head_count, DK), jnp.float32)
    states_before, priors = [], []
    for b in range(block_count):
        states_before.append(state)
        priors.append(prior)
        state = jnp.where(through[b], block_decay[b][:, :, None] * state, 0.0) + added[b]
        prior = prior * block_decay[b]
    states_before = jnp.stack(states_before)
    priors = jnp.stack(priors)
    local_state = state
    carried = (block_segment == segment_before[:, None])[:, :, None, None]
    outside = jnp.einsum(
        "bphc,bhcv->bphv", queries * jnp.exp(cumulative), states_before, precision=HIGHEST_PRECISION
    )
    attended = inside + jnp.where(carried, outside, 0.0)

    end_row = jnp.clip(offset, 0, row_count - 1)
    end_block, end_pos = end_row // BLOCK, end_row % BLOCK
    picks = jnp.arange(request_count)
    def at_end_block(array):
        chosen = array[0]
        for b in range(1, block_count):
            hit = (end_block == b).reshape((request_count,) + (1,) * (array.ndim - 1))
            chosen = jnp.where(hit, array[b][None], chosen)
        return chosen

    end_keys_rows = at_end_block(key_rows)
    end_values = at_end_block(values)
    end_cumulative = at_end_block(cumulative)
    end_segments = at_end_block(block_segment)
    end_decay = end_cumulative[picks, end_pos]
    end_segment = end_segments[picks, end_pos]
    end_allowed = (
        (indices[None, :] <= end_pos[:, None]) & (end_segments == end_segment[:, None])
    )[:, :, None, None]
    end_spread = jnp.where(end_allowed, end_decay[:, None] - end_cumulative, 0.0)
    end_weighted = jnp.where(end_allowed, end_keys_rows * jnp.exp(end_spread), 0.0).astype(
        jnp.bfloat16
    )
    within = jnp.einsum("rjhc,rjhv->rhcv", end_weighted, end_values, preferred_element_type=jnp.float32)
    end_carried = (end_segment == at_end_block(segment_before))[:, None, None, None]
    reached = jnp.where(end_carried, jnp.exp(end_decay)[:, :, :, None] * at_end_block(states_before), 0.0)
    local_ends = within + reached

    through_shard = segment[-1] == segment_prior
    decay_factor = jnp.where(through_shard, priors[-1] * block_decay[-1], 0.0)
    incoming = state_prefix(decay_factor, local_state, "seq", -(-MAXLEN // row_count))

    reach = jnp.exp(cumulative) * priors[:, None]
    from_before = (block_segment == segment_prior)[:, :, None, None]
    correction = jnp.einsum(
        "bphc,hcv->bphv",
        jnp.where(from_before, queries * reach, 0.0),
        incoming,
        precision=HIGHEST_PRECISION,
    )
    attended = (attended + correction).reshape(row_count, head_count, DV)
    end_reach = jnp.exp(end_decay) * at_end_block(priors)
    end_from_before = (end_segment == segment_prior)[:, None, None, None]
    end_states = local_ends + jnp.where(
        end_from_before, end_reach[:, :, :, None] * incoming[None], 0.0
    )
    end_states = jnp.where(owned_here[:, None, None, None], end_states, 0.0)
    edge_rows = conv_edges.reshape(request_count, head_count, -1, DV)
    payload = lax.psum(jnp.concatenate([end_states, edge_rows], axis=2), "seq")
    last_states = payload[:, :, :DK]
    conv_edges = payload[:, :, DK:].reshape(conv_edges.shape)

    gated = head_output(attended, gate_out, head_gain)
    partial = jnp.dot(gated, out_weight, preferred_element_type=jnp.float32).astype(jnp.bfloat16)
    pieces = partial.reshape(row_count, tp_size, column_count)
    arrived = [lax.dynamic_index_in_dim(pieces, tp_index, 1, keepdims=False)]
    for shift in range(1, tp_size):
        outgoing = lax.dynamic_index_in_dim(pieces, (tp_index + shift) % tp_size, 1, keepdims=False)
        arrived.append(
            lax.ppermute(outgoing, "tp", [(i, (i + shift) % tp_size) for i in range(tp_size)])
        )
    arrived = jnp.stack(arrived)
    summed = jnp.zeros((row_count, column_count), jnp.float32)
    for group in range(tp_size):
        summed = summed + lax.dynamic_index_in_dim(
            arrived, (tp_index - group) % tp_size, 0, keepdims=False
        ).astype(jnp.float32)
    column_start = tp_index * column_count
    own_columns = lax.dynamic_slice_in_dim(residual, column_start, column_count, 1)
    hidden = (own_columns + summed).astype(jnp.bfloat16)

    last_rows = jnp.where(owned_here[:, None], hidden[end_row], jnp.zeros((), jnp.bfloat16))
    placed = lax.dynamic_update_slice_in_dim(
        jnp.zeros((request_count, tokens.shape[1]), jnp.bfloat16), last_rows, column_start, 1
    )
    full_rows = butterfly_sum(butterfly_sum(placed, "seq"), "tp").astype(jnp.float32)
    mean_square = jnp.mean(full_rows * full_rows, axis=1)
    last_norms = jnp.sqrt(mean_square)
    final_rows = (full_rows * lax.rsqrt(mean_square[:, None] + 1e-06) * final_gain).astype(
        jnp.bfloat16
    )
    logits = jnp.dot(final_rows, embedding.T, preferred_element_type=jnp.float32)
    max_logits = jnp.max(logits, axis=1, keepdims=True)
    return (hidden, last_states, conv_edges, last_norms, max_logits)


def solution(mesh):
    in_specs = (
        P("seq", None),
        P(),
        P(None, "tp"),
        P(None, "tp"),
        P(),
        P(None, "tp"),
        P("tp"),
        P(None, "tp"),
        P(),
        P("tp", None),
        P(),
        P(("seq", "tp"), None),
        P(),
        P(),
    )
    out_specs = (
        P("seq", "tp"),
        P(None, "tp", None, None),
        P(None, None, "tp"),
        P(),
        P(None, ("seq", "tp")),
    )
    return jax.shard_map(shards, mesh=mesh, in_specs=in_specs, out_specs=out_specs, check_vma=False)
```

```python
import jax
import jax.numpy as jnp
from jax import lax
from jax.sharding import PartitionSpec as P

DK = 256
DV = 512
KCONV = 4
BLOCK = 64
MAXLEN = 4096


HIGHEST_PRECISION = lax.Precision.HIGHEST


def passed_along(array, axis, by):
    peers = lax.axis_size(axis)
    pairs = [(i, i + by) for i in range(peers) if 0 <= i + by < peers]
    return lax.ppermute(array, axis, pairs)


def butterfly_sum(array, axis):
    peers = lax.axis_size(axis)
    step = 1
    while step < peers:
        pairs = [(i, i ^ step) for i in range(peers)]
        array = array + lax.ppermute(array, axis, pairs)
        step *= 2
    return array


def send_pair(decay, state, axis, by):
    high = decay.astype(jnp.bfloat16)
    low = (decay - high.astype(jnp.float32)).astype(jnp.bfloat16)
    row = jnp.concatenate([high, low], axis=-1)[:, None, :]
    packed = jnp.concatenate([state.astype(jnp.bfloat16), row], axis=1)
    got = passed_along(packed, axis, by)
    tail = got[:, DK].astype(jnp.float32)
    return tail[:, :DK] + tail[:, DK:], got[:, :DK].astype(jnp.float32)


def state_prefix(decay_factor, local_state, axis, reach):
    peers, place = lax.axis_size(axis), lax.axis_index(axis)
    decay, state = send_pair(decay_factor, local_state, axis, 1)
    step = 1
    while step < min(peers, reach):
        earlier_decay, earlier_state = send_pair(decay, state, axis, step)
        state = state + decay[..., None] * earlier_state
        decay = jnp.where(place >= step, decay * earlier_decay, decay)
        step *= 2
    return state


def segments(lengths, packed_order, positions):
    request_count = lengths.shape[0]
    select = (packed_order[:, None] == jnp.arange(request_count, dtype=jnp.int32)[None, :]).astype(
        jnp.int32
    )
    packed_len = jnp.sum(select * lengths[None, :], axis=1)
    end_points = jnp.cumsum(packed_len)
    starts = end_points - packed_len
    segment = jnp.sum((positions[:, None] >= starts[None, :]).astype(jnp.int32), axis=1) - 1
    last_index = jnp.sum(select * (end_points - 1)[:, None], axis=0)
    return (segment, last_index)


def causal_conv(padded, padded_segment, conv_weight, row_count):
    running = jnp.zeros((row_count, padded.shape[1]), jnp.float32)
    current = padded_segment[KCONV - 1 :]
    for offset in range(KCONV):
        window = padded[offset : offset + row_count]
        same_segment = (padded_segment[offset : offset + row_count] == current)[:, None]
        running = running + jnp.where(same_segment, window, 0.0) * conv_weight[offset]
    return running


def activate(convolved, head_count):
    shaped = convolved.reshape(convolved.shape[0], head_count, 2 * DK + DV)
    channel = jnp.arange(2 * DK + DV)
    return jnp.where(channel < 2 * DK, jax.nn.silu(shaped), shaped).astype(jnp.bfloat16)


def head_output(attended, gate_out, head_gain):
    row_count, head_count, value_width = attended.shape
    mean_square = jnp.mean(attended * attended, axis=2, keepdims=True)
    gate_values = jax.nn.silu(
        gate_out.astype(jnp.float32).reshape(row_count, head_count, value_width)
    )
    gated = attended * lax.rsqrt(mean_square + 1e-05) * head_gain * gate_values
    return gated.reshape(row_count, head_count * value_width).astype(jnp.bfloat16)


def shards(
    tokens,
    norm_gain,
    qkv_weight,
    conv_weight,
    gate_down,
    gate_up,
    gate_bias,
    out_gate_weight,
    head_gain,
    out_weight,
    final_gain,
    embedding,
    lengths,
    packed_order,
):
    row_count = tokens.shape[0]
    head_count = out_weight.shape[0] // DV
    tp_size = lax.axis_size("tp")
    tp_index = lax.axis_index("tp")
    column_count = tokens.shape[1] // tp_size
    request_count = lengths.shape[0]
    start_row = lax.axis_index("seq") * row_count
    positions = start_row + jnp.arange(-(KCONV - 1), row_count, dtype=jnp.int32)
    segment_all, last_index = segments(lengths, packed_order, positions)
    segment = segment_all[KCONV - 1 :]
    segment_prior = segment_all[KCONV - 2]
    first_index = last_index - lengths + 1
    residual = tokens.astype(jnp.float32)
    normed = (
        residual
        * lax.rsqrt(jnp.mean(residual * residual, axis=1, keepdims=True) + 1e-06)
        * norm_gain
    ).astype(jnp.bfloat16)
    projected = jnp.dot(normed, qkv_weight, preferred_element_type=jnp.float32).astype(jnp.bfloat16)
    rim_rows = passed_along(projected[row_count - (KCONV - 1) :], "seq", 1)
    padded = jnp.concatenate([rim_rows, projected], axis=0)
    convolved = causal_conv(padded.astype(jnp.float32), segment_all, conv_weight, row_count)
    activated = activate(convolved, head_count)
    lowrank = jnp.dot(normed, gate_down, preferred_element_type=jnp.float32)
    gate_logits = (
        jnp.dot(lowrank, gate_up.astype(jnp.float32), precision=HIGHEST_PRECISION) + gate_bias
    )
    decays = (jax.nn.log_sigmoid(gate_logits) / 16.0).reshape(row_count, head_count, DK)
    gate_out = jnp.dot(normed, out_gate_weight, preferred_element_type=jnp.float32).astype(
        jnp.bfloat16
    )

    offset = last_index - start_row
    owned_here = (offset >= 0) & (offset < row_count)
    taps = jnp.arange(KCONV - 1)
    located = last_index[:, None] - (KCONV - 2) + taps[None, :]
    inside = owned_here[:, None] & (located >= first_index[:, None])
    row_of = jnp.clip(located - start_row + KCONV - 1, 0, row_count + KCONV - 2)
    one_hot = (
        row_of.reshape(-1, 1) == jnp.arange(row_count + KCONV - 1)[None, :]
    ).astype(jnp.bfloat16)
    picked = jnp.dot(one_hot, padded, preferred_element_type=jnp.float32)
    conv_edges = jnp.where(
        inside[:, :, None], picked.reshape(request_count, KCONV - 1, -1), 0.0
    )

    block_count = row_count // BLOCK
    queries = activated[:, :, :DK].astype(jnp.float32).reshape(block_count, BLOCK, head_count, DK)
    key_rows = activated[:, :, DK : 2 * DK].astype(jnp.float32).reshape(
        block_count, BLOCK, head_count, DK
    )
    values = activated[:, :, 2 * DK :].reshape(block_count, BLOCK, head_count, DV)
    block_segment = segment.reshape(block_count, BLOCK)
    segment_before = segment_all[KCONV - 2 : KCONV - 2 + row_count : BLOCK]
    cumulative = jnp.cumsum(decays.reshape(block_count, BLOCK, head_count, DK), axis=1)
    indices = jnp.arange(BLOCK)
    causal = (indices[None, :] <= indices[:, None])[None] & (
        block_segment[:, None, :] == block_segment[:, :, None]
    )
    allowed = causal[:, :, :, None, None]
    spread = jnp.where(allowed, cumulative[:, :, None] - cumulative[:, None, :], 0.0)
    weights = jnp.where(allowed, jnp.exp(spread), 0.0)
    scores = jnp.sum(queries[:, :, None] * key_rows[:, None, :] * weights, axis=-1).astype(
        jnp.bfloat16
    )
    inside = jnp.einsum("bpqh,bqhv->bphv", scores, values, preferred_element_type=jnp.float32)

    same_tail = (block_segment == block_segment[:, -1:])[:, :, None, None]
    scaled = jnp.where(
        same_tail, key_rows * jnp.exp(cumulative[:, -1:] - cumulative), 0.0
    ).astype(jnp.bfloat16)
    added = jnp.einsum("bjhc,bjhv->bhcv", scaled, values, preferred_element_type=jnp.float32)
    through = block_segment[:, -1] == segment_before
    block_decay = jnp.exp(cumulative[:, -1])
    state = jnp.zeros((head_count, DK, DV), jnp.float32)
    prior = jnp.ones((head_count, DK), jnp.float32)
    states_before, priors = [], []
    for b in range(block_count):
        states_before.append(state)
        priors.append(prior)
        state = jnp.where(through[b], block_decay[b][:, :, None] * state, 0.0) + added[b]
        prior = prior * block_decay[b]
    states_before = jnp.stack(states_before)
    priors = jnp.stack(priors)
    local_state = state
    carried = (block_segment == segment_before[:, None])[:, :, None, None]
    outside = jnp.einsum(
        "bphc,bhcv->bphv", queries * jnp.exp(cumulative), states_before, precision=HIGHEST_PRECISION
    )
    attended = inside + jnp.where(carried, outside, 0.0)

    end_row = jnp.clip(offset, 0, row_count - 1)
    end_block, end_pos = end_row // BLOCK, end_row % BLOCK
    picks = jnp.arange(request_count)
    def at_end_block(array):
        chosen = array[0]
        for b in range(1, block_count):
            hit = (end_block == b).reshape((request_count,) + (1,) * (array.ndim - 1))
            chosen = jnp.where(hit, array[b][None], chosen)
        return chosen

    end_keys_rows = at_end_block(key_rows)
    end_values = at_end_block(values)
    end_cumulative = at_end_block(cumulative)
    end_segments = at_end_block(block_segment)
    end_decay = end_cumulative[picks, end_pos]
    end_segment = end_segments[picks, end_pos]
    end_allowed = (
        (indices[None, :] <= end_pos[:, None]) & (end_segments == end_segment[:, None])
    )[:, :, None, None]
    end_spread = jnp.where(end_allowed, end_decay[:, None] - end_cumulative, 0.0)
    end_weighted = jnp.where(end_allowed, end_keys_rows * jnp.exp(end_spread), 0.0).astype(
        jnp.bfloat16
    )
    within = jnp.einsum("rjhc,rjhv->rhcv", end_weighted, end_values, preferred_element_type=jnp.float32)
    end_carried = (end_segment == at_end_block(segment_before))[:, None, None, None]
    reached = jnp.where(end_carried, jnp.exp(end_decay)[:, :, :, None] * at_end_block(states_before), 0.0)
    local_ends = within + reached

    through_shard = segment[-1] == segment_prior
    decay_factor = jnp.where(through_shard, priors[-1] * block_decay[-1], 0.0)
    incoming = state_prefix(decay_factor, local_state, "seq", -(-MAXLEN // row_count))

    reach = jnp.exp(cumulative) * priors[:, None]
    from_before = (block_segment == segment_prior)[:, :, None, None]
    correction = jnp.einsum(
        "bphc,hcv->bphv",
        jnp.where(from_before, queries * reach, 0.0),
        incoming,
        precision=HIGHEST_PRECISION,
    )
    attended = (attended + correction).reshape(row_count, head_count, DV)
    end_reach = jnp.exp(end_decay) * at_end_block(priors)
    end_from_before = (end_segment == segment_prior)[:, None, None, None]
    end_states = local_ends + jnp.where(
        end_from_before, end_reach[:, :, :, None] * incoming[None], 0.0
    )
    end_states = jnp.where(owned_here[:, None, None, None], end_states, 0.0)
    edge_rows = conv_edges.reshape(request_count, head_count, -1, DV)
    payload = lax.psum(jnp.concatenate([end_states, edge_rows], axis=2), "seq")
    last_states = payload[:, :, :DK]
    conv_edges = payload[:, :, DK:].reshape(conv_edges.shape)

    gated = head_output(attended, gate_out, head_gain)
    partial = jnp.dot(gated, out_weight, preferred_element_type=jnp.float32).astype(jnp.bfloat16)
    pieces = partial.reshape(row_count, tp_size, column_count)
    arrived = [lax.dynamic_index_in_dim(pieces, tp_index, 1, keepdims=False)]
    for shift in range(1, tp_size):
        outgoing = lax.dynamic_index_in_dim(pieces, (tp_index + shift) % tp_size, 1, keepdims=False)
        arrived.append(
            lax.ppermute(outgoing, "tp", [(i, (i + shift) % tp_size) for i in range(tp_size)])
        )
    arrived = jnp.stack(arrived)
    summed = jnp.zeros((row_count, column_count), jnp.float32)
    for group in range(tp_size):
        summed = summed + lax.dynamic_index_in_dim(
            arrived, (tp_index - group) % tp_size, 0, keepdims=False
        ).astype(jnp.float32)
    column_start = tp_index * column_count
    own_columns = lax.dynamic_slice_in_dim(residual, column_start, column_count, 1)
    hidden = (own_columns + summed).astype(jnp.bfloat16)

    last_rows = jnp.where(owned_here[:, None], hidden[end_row], jnp.zeros((), jnp.bfloat16))
    placed = lax.dynamic_update_slice_in_dim(
        jnp.zeros((request_count, tokens.shape[1]), jnp.bfloat16), last_rows, column_start, 1
    )
    full_rows = butterfly_sum(butterfly_sum(placed, "seq"), "tp").astype(jnp.float32)
    mean_square = jnp.mean(full_rows * full_rows, axis=1)
    last_norms = jnp.sqrt(mean_square)
    final_rows = (full_rows * lax.rsqrt(mean_square[:, None] + 1e-06) * final_gain).astype(
        jnp.bfloat16
    )
    logits = jnp.dot(final_rows, embedding.T, preferred_element_type=jnp.float32)
    max_logits = jnp.max(logits, axis=1, keepdims=True)
    return (hidden, last_states, conv_edges, last_norms, max_logits)


def solution(mesh):
    in_specs = (
        P("seq", None),
        P(),
        P(None, "tp"),
        P(None, "tp"),
        P(),
        P(None, "tp"),
        P("tp"),
        P(None, "tp"),
        P(),
        P("tp", None),
        P(),
        P(("seq", "tp"), None),
        P(),
        P(),
    )
    out_specs = (
        P("seq", "tp"),
        P(None, "tp", None, None),
        P(None, None, "tp"),
        P(),
        P(None, ("seq", "tp")),
    )
    return jax.shard_map(shards, mesh=mesh, in_specs=in_specs, out_specs=out_specs, check_vma=False)
```

```python
import jax
import jax.numpy as jnp
from jax import lax
from jax.sharding import PartitionSpec as P

DK = 256
DV = 512
KCONV = 4
BLOCK = 64
MAXLEN = 4096


HIGHEST_PRECISION = lax.Precision.HIGHEST


def passed_along(array, axis, by):
    peers = lax.axis_size(axis)
    pairs = [(i, i + by) for i in range(peers) if 0 <= i + by < peers]
    return lax.ppermute(array, axis, pairs)


def butterfly_sum(array, axis):
    peers = lax.axis_size(axis)
    step = 1
    while step < peers:
        pairs = [(i, i ^ step) for i in range(peers)]
        array = array + lax.ppermute(array, axis, pairs)
        step *= 2
    return array


def send_pair(decay, state, axis, by):
    high = decay.astype(jnp.bfloat16)
    low = (decay - high.astype(jnp.float32)).astype(jnp.bfloat16)
    row = jnp.concatenate([high, low], axis=-1)[:, None, :]
    packed = jnp.concatenate([state.astype(jnp.bfloat16), row], axis=1)
    got = passed_along(packed, axis, by)
    tail = got[:, DK].astype(jnp.float32)
    return tail[:, :DK] + tail[:, DK:], got[:, :DK].astype(jnp.float32)


def state_prefix(decay_factor, local_state, axis, reach, companion):
    peers, place = lax.axis_size(axis), lax.axis_index(axis)
    decay, state = send_pair(decay_factor, local_state, axis, 1)
    companion, decay, state = lax.optimization_barrier((companion, decay, state))
    step = 1
    while step < min(peers, reach):
        earlier_decay, earlier_state = send_pair(decay, state, axis, step)
        state = state + decay[..., None] * earlier_state
        decay = jnp.where(place >= step, decay * earlier_decay, decay)
        step *= 2
    return state, companion


def segments(lengths, packed_order, positions):
    request_count = lengths.shape[0]
    select = (packed_order[:, None] == jnp.arange(request_count, dtype=jnp.int32)[None, :]).astype(
        jnp.int32
    )
    packed_len = jnp.sum(select * lengths[None, :], axis=1)
    end_points = jnp.cumsum(packed_len)
    starts = end_points - packed_len
    segment = jnp.sum((positions[:, None] >= starts[None, :]).astype(jnp.int32), axis=1) - 1
    last_index = jnp.sum(select * (end_points - 1)[:, None], axis=0)
    return (segment, last_index)


def causal_conv(padded, padded_segment, conv_weight, row_count):
    running = jnp.zeros((row_count, padded.shape[1]), jnp.float32)
    current = padded_segment[KCONV - 1 :]
    for offset in range(KCONV):
        window = padded[offset : offset + row_count]
        same_segment = (padded_segment[offset : offset + row_count] == current)[:, None]
        running = running + jnp.where(same_segment, window, 0.0) * conv_weight[offset]
    return running


def activate(convolved, head_count):
    shaped = convolved.reshape(convolved.shape[0], head_count, 2 * DK + DV)
    channel = jnp.arange(2 * DK + DV)
    return jnp.where(channel < 2 * DK, jax.nn.silu(shaped), shaped).astype(jnp.bfloat16)


def head_output(attended, gate_out, head_gain):
    row_count, head_count, value_width = attended.shape
    mean_square = jnp.mean(attended * attended, axis=2, keepdims=True)
    gate_values = jax.nn.silu(
        gate_out.astype(jnp.float32).reshape(row_count, head_count, value_width)
    )
    gated = attended * lax.rsqrt(mean_square + 1e-05) * head_gain * gate_values
    return gated.reshape(row_count, head_count * value_width).astype(jnp.bfloat16)


def shards(
    tokens,
    norm_gain,
    qkv_weight,
    conv_weight,
    gate_down,
    gate_up,
    gate_bias,
    out_gate_weight,
    head_gain,
    out_weight,
    final_gain,
    embedding,
    lengths,
    packed_order,
):
    row_count = tokens.shape[0]
    head_count = out_weight.shape[0] // DV
    tp_size = lax.axis_size("tp")
    tp_index = lax.axis_index("tp")
    column_count = tokens.shape[1] // tp_size
    request_count = lengths.shape[0]
    start_row = lax.axis_index("seq") * row_count
    positions = start_row + jnp.arange(-(KCONV - 1), row_count, dtype=jnp.int32)
    segment_all, last_index = segments(lengths, packed_order, positions)
    segment = segment_all[KCONV - 1 :]
    segment_prior = segment_all[KCONV - 2]
    first_index = last_index - lengths + 1
    residual = tokens.astype(jnp.float32)
    normed = (
        residual
        * lax.rsqrt(jnp.mean(residual * residual, axis=1, keepdims=True) + 1e-06)
        * norm_gain
    ).astype(jnp.bfloat16)
    projected = jnp.dot(normed, qkv_weight, preferred_element_type=jnp.float32).astype(jnp.bfloat16)
    rim_rows = passed_along(projected[row_count - (KCONV - 1) :], "seq", 1)
    padded = jnp.concatenate([rim_rows, projected], axis=0)
    convolved = causal_conv(padded.astype(jnp.float32), segment_all, conv_weight, row_count)
    activated = activate(convolved, head_count)
    lowrank = jnp.dot(normed, gate_down, preferred_element_type=jnp.float32)
    gate_logits = (
        jnp.dot(lowrank, gate_up.astype(jnp.float32), precision=HIGHEST_PRECISION) + gate_bias
    )
    decays = (jax.nn.log_sigmoid(gate_logits) / 16.0).reshape(row_count, head_count, DK)
    gate_out = jnp.dot(normed, out_gate_weight, preferred_element_type=jnp.float32).astype(
        jnp.bfloat16
    )

    offset = last_index - start_row
    owned_here = (offset >= 0) & (offset < row_count)
    edge_list = []
    for tap in range(KCONV - 1):
        located = last_index - (KCONV - 2) + tap
        inside = owned_here & (located >= first_index)
        picked = padded[jnp.clip(located - start_row + KCONV - 1, 0, row_count + KCONV - 2)].astype(
            jnp.float32
        )
        edge_list.append(jnp.where(inside[:, None], picked, 0.0))
    conv_edges = jnp.stack(edge_list, axis=1)

    block_count = row_count // BLOCK
    queries = activated[:, :, :DK].astype(jnp.float32).reshape(block_count, BLOCK, head_count, DK)
    key_rows = activated[:, :, DK : 2 * DK].astype(jnp.float32).reshape(
        block_count, BLOCK, head_count, DK
    )
    values = activated[:, :, 2 * DK :].reshape(block_count, BLOCK, head_count, DV)
    block_segment = segment.reshape(block_count, BLOCK)
    segment_before = segment_all[KCONV - 2 : KCONV - 2 + row_count : BLOCK]
    cumulative = jnp.cumsum(decays.reshape(block_count, BLOCK, head_count, DK), axis=1)
    indices = jnp.arange(BLOCK)
    causal = (indices[None, :] <= indices[:, None])[None] & (
        block_segment[:, None, :] == block_segment[:, :, None]
    )
    allowed = causal[:, :, :, None, None]
    spread = jnp.where(allowed, cumulative[:, :, None] - cumulative[:, None, :], 0.0)
    weights = jnp.where(allowed, jnp.exp(spread), 0.0)
    scores = jnp.sum(queries[:, :, None] * key_rows[:, None, :] * weights, axis=-1).astype(
        jnp.bfloat16
    )
    inside = jnp.einsum("bpqh,bqhv->bphv", scores, values, preferred_element_type=jnp.float32)

    same_tail = (block_segment == block_segment[:, -1:])[:, :, None, None]
    scaled = jnp.where(
        same_tail, key_rows * jnp.exp(cumulative[:, -1:] - cumulative), 0.0
    ).astype(jnp.bfloat16)
    added = jnp.einsum("bjhc,bjhv->bhcv", scaled, values, preferred_element_type=jnp.float32)
    through = block_segment[:, -1] == segment_before
    block_decay = jnp.exp(cumulative[:, -1])
    state = jnp.zeros((head_count, DK, DV), jnp.float32)
    prior = jnp.ones((head_count, DK), jnp.float32)
    states_before, priors = [], []
    for b in range(block_count):
        states_before.append(state)
        priors.append(prior)
        state = jnp.where(through[b], block_decay[b][:, :, None] * state, 0.0) + added[b]
        prior = prior * block_decay[b]
    states_before = jnp.stack(states_before)
    priors = jnp.stack(priors)
    local_state = state
    carried = (block_segment == segment_before[:, None])[:, :, None, None]
    outside = jnp.einsum(
        "bphc,bhcv->bphv", queries * jnp.exp(cumulative), states_before, precision=HIGHEST_PRECISION
    )
    attended = inside + jnp.where(carried, outside, 0.0)

    end_row = jnp.clip(offset, 0, row_count - 1)
    end_block, end_pos = end_row // BLOCK, end_row % BLOCK
    picks = jnp.arange(request_count)
    def at_end_block(array):
        chosen = array[0]
        for b in range(1, block_count):
            hit = (end_block == b).reshape((request_count,) + (1,) * (array.ndim - 1))
            chosen = jnp.where(hit, array[b][None], chosen)
        return chosen

    end_keys_rows = at_end_block(key_rows)
    end_values = at_end_block(values)
    end_cumulative = at_end_block(cumulative)
    end_segments = at_end_block(block_segment)
    end_decay = end_cumulative[picks, end_pos]
    end_segment = end_segments[picks, end_pos]
    end_allowed = (
        (indices[None, :] <= end_pos[:, None]) & (end_segments == end_segment[:, None])
    )[:, :, None, None]
    end_spread = jnp.where(end_allowed, end_decay[:, None] - end_cumulative, 0.0)
    end_weighted = jnp.where(end_allowed, end_keys_rows * jnp.exp(end_spread), 0.0).astype(
        jnp.bfloat16
    )
    within = jnp.einsum("rjhc,rjhv->rhcv", end_weighted, end_values, preferred_element_type=jnp.float32)
    end_carried = (end_segment == at_end_block(segment_before))[:, None, None, None]
    reached = jnp.where(end_carried, jnp.exp(end_decay)[:, :, :, None] * at_end_block(states_before), 0.0)
    local_ends = within + reached

    through_shard = segment[-1] == segment_prior
    decay_factor = jnp.where(through_shard, priors[-1] * block_decay[-1], 0.0)
    incoming, local_ends = state_prefix(
        decay_factor, local_state, "seq", -(-MAXLEN // row_count), local_ends
    )

    reach = jnp.exp(cumulative) * priors[:, None]
    from_before = (block_segment == segment_prior)[:, :, None, None]
    correction = jnp.einsum(
        "bphc,hcv->bphv",
        jnp.where(from_before, queries * reach, 0.0),
        incoming,
        precision=HIGHEST_PRECISION,
    )
    attended = (attended + correction).reshape(row_count, head_count, DV)
    end_reach = jnp.exp(end_decay) * at_end_block(priors)
    end_from_before = (end_segment == segment_prior)[:, None, None, None]
    end_states = local_ends + jnp.where(
        end_from_before, end_reach[:, :, :, None] * incoming[None], 0.0
    )
    end_states = jnp.where(owned_here[:, None, None, None], end_states, 0.0)
    edge_rows = conv_edges.reshape(request_count, head_count, -1, DV)
    payload = lax.psum(jnp.concatenate([end_states, edge_rows], axis=2), "seq")
    last_states = payload[:, :, :DK]
    conv_edges = payload[:, :, DK:].reshape(conv_edges.shape)

    gated = head_output(attended, gate_out, head_gain)
    partial = jnp.dot(gated, out_weight, preferred_element_type=jnp.float32).astype(jnp.bfloat16)
    pieces = partial.reshape(row_count, tp_size, column_count)
    arrived = [lax.dynamic_index_in_dim(pieces, tp_index, 1, keepdims=False)]
    for shift in range(1, tp_size):
        outgoing = lax.dynamic_index_in_dim(pieces, (tp_index + shift) % tp_size, 1, keepdims=False)
        arrived.append(
            lax.ppermute(outgoing, "tp", [(i, (i + shift) % tp_size) for i in range(tp_size)])
        )
    arrived = jnp.stack(arrived)
    summed = jnp.zeros((row_count, column_count), jnp.float32)
    for group in range(tp_size):
        summed = summed + lax.dynamic_index_in_dim(
            arrived, (tp_index - group) % tp_size, 0, keepdims=False
        ).astype(jnp.float32)
    column_start = tp_index * column_count
    own_columns = lax.dynamic_slice_in_dim(residual, column_start, column_count, 1)
    hidden = (own_columns + summed).astype(jnp.bfloat16)

    last_rows = jnp.where(owned_here[:, None], hidden[end_row], jnp.zeros((), jnp.bfloat16))
    placed = lax.dynamic_update_slice_in_dim(
        jnp.zeros((request_count, tokens.shape[1]), jnp.bfloat16), last_rows, column_start, 1
    )
    full_rows = butterfly_sum(butterfly_sum(placed, "seq"), "tp").astype(jnp.float32)
    mean_square = jnp.mean(full_rows * full_rows, axis=1)
    last_norms = jnp.sqrt(mean_square)
    final_rows = (full_rows * lax.rsqrt(mean_square[:, None] + 1e-06) * final_gain).astype(
        jnp.bfloat16
    )
    logits = jnp.dot(final_rows, embedding.T, preferred_element_type=jnp.float32)
    max_logits = jnp.max(logits, axis=1, keepdims=True)
    return (hidden, last_states, conv_edges, last_norms, max_logits)


def solution(mesh):
    in_specs = (
        P("seq", None),
        P(),
        P(None, "tp"),
        P(None, "tp"),
        P(),
        P(None, "tp"),
        P("tp"),
        P(None, "tp"),
        P(),
        P("tp", None),
        P(),
        P(("seq", "tp"), None),
        P(),
        P(),
    )
    out_specs = (
        P("seq", "tp"),
        P(None, "tp", None, None),
        P(None, None, "tp"),
        P(),
        P(None, ("seq", "tp")),
    )
    return jax.shard_map(shards, mesh=mesh, in_specs=in_specs, out_specs=out_specs, check_vma=False)
```

```python
import jax
import jax.numpy as jnp
from jax import lax
from jax.sharding import PartitionSpec as P

DK = 256
DV = 512
KCONV = 4
BLOCK = 64
MAXLEN = 4096


HIGHEST_PRECISION = lax.Precision.HIGHEST


def passed_along(array, axis, by):
    peers = lax.axis_size(axis)
    pairs = [(i, i + by) for i in range(peers) if 0 <= i + by < peers]
    return lax.ppermute(array, axis, pairs)


def butterfly_sum(array, axis):
    peers = lax.axis_size(axis)
    step = 1
    while step < peers:
        pairs = [(i, i ^ step) for i in range(peers)]
        array = array + lax.ppermute(array, axis, pairs)
        step *= 2
    return array


def send_pair(decay, state, axis, by):
    high = decay.astype(jnp.bfloat16)
    low = (decay - high.astype(jnp.float32)).astype(jnp.bfloat16)
    row = jnp.concatenate([high, low], axis=-1)[:, None, :]
    packed = jnp.concatenate([state.astype(jnp.bfloat16), row], axis=1)
    got = passed_along(packed, axis, by)
    tail = got[:, DK].astype(jnp.float32)
    return tail[:, :DK] + tail[:, DK:], got[:, :DK].astype(jnp.float32)


def state_prefix(decay_factor, local_state, axis, reach):
    peers, place = lax.axis_size(axis), lax.axis_index(axis)
    decay, state = send_pair(decay_factor, local_state, axis, 1)
    step = 1
    while step < min(peers, reach):
        earlier_decay, earlier_state = send_pair(decay, state, axis, step)
        state = state + decay[..., None] * earlier_state
        decay = jnp.where(place >= step, decay * earlier_decay, decay)
        step *= 2
    return state


def segments(lengths, packed_order, positions):
    request_count = lengths.shape[0]
    select = (packed_order[:, None] == jnp.arange(request_count, dtype=jnp.int32)[None, :]).astype(
        jnp.int32
    )
    packed_len = jnp.sum(select * lengths[None, :], axis=1)
    end_points = jnp.cumsum(packed_len)
    starts = end_points - packed_len
    segment = jnp.sum((positions[:, None] >= starts[None, :]).astype(jnp.int32), axis=1) - 1
    last_index = jnp.sum(select * (end_points - 1)[:, None], axis=0)
    return (segment, last_index)


def causal_conv(padded, padded_segment, conv_weight, row_count):
    running = jnp.zeros((row_count, padded.shape[1]), jnp.float32)
    current = padded_segment[KCONV - 1 :]
    for offset in range(KCONV):
        window = padded[offset : offset + row_count]
        same_segment = (padded_segment[offset : offset + row_count] == current)[:, None]
        running = running + jnp.where(same_segment, window, 0.0) * conv_weight[offset]
    return running


def activate(convolved, head_count):
    shaped = convolved.reshape(convolved.shape[0], head_count, 2 * DK + DV)
    channel = jnp.arange(2 * DK + DV)
    return jnp.where(channel < 2 * DK, jax.nn.silu(shaped), shaped).astype(jnp.bfloat16)


def head_output(attended, gate_out, head_gain):
    row_count, head_count, value_width = attended.shape
    mean_square = jnp.mean(attended * attended, axis=2, keepdims=True)
    gate_values = jax.nn.silu(
        gate_out.astype(jnp.float32).reshape(row_count, head_count, value_width)
    )
    gated = attended * lax.rsqrt(mean_square + 1e-05) * head_gain * gate_values
    return gated.reshape(row_count, head_count * value_width).astype(jnp.bfloat16)


def shards(
    tokens,
    norm_gain,
    qkv_weight,
    conv_weight,
    gate_down,
    gate_up,
    gate_bias,
    out_gate_weight,
    head_gain,
    out_weight,
    final_gain,
    embedding,
    lengths,
    packed_order,
):
    row_count = tokens.shape[0]
    head_count = out_weight.shape[0] // DV
    tp_size = lax.axis_size("tp")
    tp_index = lax.axis_index("tp")
    column_count = tokens.shape[1] // tp_size
    request_count = lengths.shape[0]
    start_row = lax.axis_index("seq") * row_count
    positions = start_row + jnp.arange(-(KCONV - 1), row_count, dtype=jnp.int32)
    segment_all, last_index = segments(lengths, packed_order, positions)
    segment = segment_all[KCONV - 1 :]
    segment_prior = segment_all[KCONV - 2]
    first_index = last_index - lengths + 1
    residual = tokens.astype(jnp.float32)
    normed = (
        residual
        * lax.rsqrt(jnp.mean(residual * residual, axis=1, keepdims=True) + 1e-06)
        * norm_gain
    ).astype(jnp.bfloat16)
    projected = jnp.dot(normed, qkv_weight, preferred_element_type=jnp.float32).astype(jnp.bfloat16)
    rim_rows = passed_along(projected[row_count - (KCONV - 1) :], "seq", 1)
    padded = jnp.concatenate([rim_rows, projected], axis=0)
    convolved = causal_conv(padded.astype(jnp.float32), segment_all, conv_weight, row_count)
    activated = activate(convolved, head_count)
    lowrank = jnp.dot(normed, gate_down, preferred_element_type=jnp.float32)
    gate_logits = (
        jnp.dot(lowrank, gate_up.astype(jnp.float32), precision=HIGHEST_PRECISION) + gate_bias
    )
    decays = (jax.nn.log_sigmoid(gate_logits) / 16.0).reshape(row_count, head_count, DK)
    gate_out = jnp.dot(normed, out_gate_weight, preferred_element_type=jnp.float32).astype(
        jnp.bfloat16
    )

    offset = last_index - start_row
    owned_here = (offset >= 0) & (offset < row_count)
    edge_list = []
    for tap in range(KCONV - 1):
        located = last_index - (KCONV - 2) + tap
        inside = owned_here & (located >= first_index)
        picked = padded[jnp.clip(located - start_row + KCONV - 1, 0, row_count + KCONV - 2)].astype(
            jnp.float32
        )
        edge_list.append(jnp.where(inside[:, None], picked, 0.0))
    conv_edges = jnp.stack(edge_list, axis=1)

    block_count = row_count // BLOCK
    queries = activated[:, :, :DK].astype(jnp.float32).reshape(block_count, BLOCK, head_count, DK)
    key_rows = activated[:, :, DK : 2 * DK].astype(jnp.float32).reshape(
        block_count, BLOCK, head_count, DK
    )
    values = activated[:, :, 2 * DK :].reshape(block_count, BLOCK, head_count, DV)
    block_segment = segment.reshape(block_count, BLOCK)
    segment_before = segment_all[KCONV - 2 : KCONV - 2 + row_count : BLOCK]
    cumulative = jnp.cumsum(decays.reshape(block_count, BLOCK, head_count, DK), axis=1)
    indices = jnp.arange(BLOCK)
    half = BLOCK // 2

    def score_part(rows, cols, diagonal):
        allowed = block_segment[:, rows, None] == block_segment[:, None, cols]
        if diagonal:
            allowed = allowed & (indices[None, :half] <= indices[:half, None])[None]
        allowed = allowed[:, :, :, None, None]
        spread = jnp.where(
            allowed, cumulative[:, rows][:, :, None] - cumulative[:, cols][:, None, :], 0.0
        )
        weights = jnp.where(allowed, jnp.exp(spread), 0.0)
        return jnp.sum(
            queries[:, rows][:, :, None] * key_rows[:, cols][:, None, :] * weights, axis=-1
        )

    first, second = slice(0, half), slice(half, BLOCK)
    upper = score_part(first, first, True)
    scores = jnp.concatenate(
        [
            jnp.concatenate([upper, jnp.zeros_like(upper)], axis=2),
            jnp.concatenate([score_part(second, first, False), score_part(second, second, True)], axis=2),
        ],
        axis=1,
    ).astype(jnp.bfloat16)
    inside = jnp.einsum("bpqh,bqhv->bphv", scores, values, preferred_element_type=jnp.float32)

    same_tail = (block_segment == block_segment[:, -1:])[:, :, None, None]
    scaled = jnp.where(
        same_tail, key_rows * jnp.exp(cumulative[:, -1:] - cumulative), 0.0
    ).astype(jnp.bfloat16)
    added = jnp.einsum("bjhc,bjhv->bhcv", scaled, values, preferred_element_type=jnp.float32)
    through = block_segment[:, -1] == segment_before
    block_decay = jnp.exp(cumulative[:, -1])
    state = jnp.zeros((head_count, DK, DV), jnp.float32)
    prior = jnp.ones((head_count, DK), jnp.float32)
    states_before, priors = [], []
    for b in range(block_count):
        states_before.append(state)
        priors.append(prior)
        state = jnp.where(through[b], block_decay[b][:, :, None] * state, 0.0) + added[b]
        prior = prior * block_decay[b]
    states_before = jnp.stack(states_before)
    priors = jnp.stack(priors)
    local_state = state
    carried = (block_segment == segment_before[:, None])[:, :, None, None]
    outside = jnp.einsum(
        "bphc,bhcv->bphv", queries * jnp.exp(cumulative), states_before, precision=HIGHEST_PRECISION
    )
    attended = inside + jnp.where(carried, outside, 0.0)

    end_row = jnp.clip(offset, 0, row_count - 1)
    end_block, end_pos = end_row // BLOCK, end_row % BLOCK
    picks = jnp.arange(request_count)
    def at_end_block(array):
        chosen = array[0]
        for b in range(1, block_count):
            hit = (end_block == b).reshape((request_count,) + (1,) * (array.ndim - 1))
            chosen = jnp.where(hit, array[b][None], chosen)
        return chosen

    end_keys_rows = at_end_block(key_rows)
    end_values = at_end_block(values)
    end_cumulative = at_end_block(cumulative)
    end_segments = at_end_block(block_segment)
    end_decay = end_cumulative[picks, end_pos]
    end_segment = end_segments[picks, end_pos]
    end_allowed = (
        (indices[None, :] <= end_pos[:, None]) & (end_segments == end_segment[:, None])
    )[:, :, None, None]
    end_spread = jnp.where(end_allowed, end_decay[:, None] - end_cumulative, 0.0)
    end_weighted = jnp.where(end_allowed, end_keys_rows * jnp.exp(end_spread), 0.0).astype(
        jnp.bfloat16
    )
    within = jnp.einsum("rjhc,rjhv->rhcv", end_weighted, end_values, preferred_element_type=jnp.float32)
    end_carried = (end_segment == at_end_block(segment_before))[:, None, None, None]
    reached = jnp.where(end_carried, jnp.exp(end_decay)[:, :, :, None] * at_end_block(states_before), 0.0)
    local_ends = within + reached

    through_shard = segment[-1] == segment_prior
    decay_factor = jnp.where(through_shard, priors[-1] * block_decay[-1], 0.0)
    incoming = state_prefix(decay_factor, local_state, "seq", -(-MAXLEN // row_count))

    reach = jnp.exp(cumulative) * priors[:, None]
    from_before = (block_segment == segment_prior)[:, :, None, None]
    correction = jnp.einsum(
        "bphc,hcv->bphv",
        jnp.where(from_before, queries * reach, 0.0),
        incoming,
        precision=HIGHEST_PRECISION,
    )
    attended = (attended + correction).reshape(row_count, head_count, DV)
    end_reach = jnp.exp(end_decay) * at_end_block(priors)
    end_from_before = (end_segment == segment_prior)[:, None, None, None]
    end_states = local_ends + jnp.where(
        end_from_before, end_reach[:, :, :, None] * incoming[None], 0.0
    )
    end_states = jnp.where(owned_here[:, None, None, None], end_states, 0.0)
    edge_rows = conv_edges.reshape(request_count, head_count, -1, DV)
    payload = lax.psum(jnp.concatenate([end_states, edge_rows], axis=2), "seq")
    last_states = payload[:, :, :DK]
    conv_edges = payload[:, :, DK:].reshape(conv_edges.shape)

    gated = head_output(attended, gate_out, head_gain)
    partial = jnp.dot(gated, out_weight, preferred_element_type=jnp.float32).astype(jnp.bfloat16)
    pieces = partial.reshape(row_count, tp_size, column_count)
    arrived = [lax.dynamic_index_in_dim(pieces, tp_index, 1, keepdims=False)]
    for shift in range(1, tp_size):
        outgoing = lax.dynamic_index_in_dim(pieces, (tp_index + shift) % tp_size, 1, keepdims=False)
        arrived.append(
            lax.ppermute(outgoing, "tp", [(i, (i + shift) % tp_size) for i in range(tp_size)])
        )
    arrived = jnp.stack(arrived)
    summed = jnp.zeros((row_count, column_count), jnp.float32)
    for group in range(tp_size):
        summed = summed + lax.dynamic_index_in_dim(
            arrived, (tp_index - group) % tp_size, 0, keepdims=False
        ).astype(jnp.float32)
    column_start = tp_index * column_count
    own_columns = lax.dynamic_slice_in_dim(residual, column_start, column_count, 1)
    hidden = (own_columns + summed).astype(jnp.bfloat16)

    last_rows = jnp.where(owned_here[:, None], hidden[end_row], jnp.zeros((), jnp.bfloat16))
    placed = lax.dynamic_update_slice_in_dim(
        jnp.zeros((request_count, tokens.shape[1]), jnp.bfloat16), last_rows, column_start, 1
    )
    full_rows = butterfly_sum(butterfly_sum(placed, "seq"), "tp").astype(jnp.float32)
    mean_square = jnp.mean(full_rows * full_rows, axis=1)
    last_norms = jnp.sqrt(mean_square)
    final_rows = (full_rows * lax.rsqrt(mean_square[:, None] + 1e-06) * final_gain).astype(
        jnp.bfloat16
    )
    logits = jnp.dot(final_rows, embedding.T, preferred_element_type=jnp.float32)
    max_logits = jnp.max(logits, axis=1, keepdims=True)
    return (hidden, last_states, conv_edges, last_norms, max_logits)


def solution(mesh):
    in_specs = (
        P("seq", None),
        P(),
        P(None, "tp"),
        P(None, "tp"),
        P(),
        P(None, "tp"),
        P("tp"),
        P(None, "tp"),
        P(),
        P("tp", None),
        P(),
        P(("seq", "tp"), None),
        P(),
        P(),
    )
    out_specs = (
        P("seq", "tp"),
        P(None, "tp", None, None),
        P(None, None, "tp"),
        P(),
        P(None, ("seq", "tp")),
    )
    return jax.shard_map(shards, mesh=mesh, in_specs=in_specs, out_specs=out_specs, check_vma=False)
```
